128 devices in a mesh: chan: 16 (over z, x_lo, core), freq: 8 (over x_hi, y).
Axes of the slice: x: 4 (x_hi: 2, x_lo: 2; x = x_hi * 2 + x_lo), y: 4, z: 4, core: 2. Of those that a mesh axis runs over, the one named last changes fastest.
Arguments:
- records: bfloat16 [67584, 8192], P('freq', 'chan')
- offsets: int32 [512], P('freq'), may hold values from 0 to 8192, as said below
- dead_mask: int32 [8192], P('chan'), may hold values 0 or 1
- band_blocks: int32 [16], P('chan'), may hold values from 0 to 2, as said below
Outputs:
- cross: bfloat16 [3, 32, 8192, 1024], P(None, 'freq', 'chan')
The draws below stay inside these ranges and needn't reach their ends.
Inputs may be any that keep to these rules, and one draw needn't show every extreme that they name: offsets[s] is the first sample of segment s within time block s // 64 of 8448 samples; all 256 samples of the segment lie in that block. band_blocks[b] is the largest block offset whose cross-spectra are kept for channel block b.
All inputs are finite; a program needn't handle non-finite values. No bound on the sum of `dead_mask` on one device may be relied on, other than what follows from the above.
Results may differ from the reference program's by a relative error of at most 0.0055.
Values may be sent and summed in bfloat16 or wider, within the bound.
No kernel may reach another device: no remote copies, remote signals or barrier semaphores. Data moves between devices by JAX's collectives and lax.ppermute only.
A program may use at most 128 MiB of HBM per device.

```python
import math
import jax
import jax.numpy as jnp
from jax import lax

CB = 512
SEG_LEN = 256
BINS = 32
FIRST_BIN = 2
BAND = 2
SEG_DEV = 64
SEGMENTS = 512
RECORD_DEV = 8448
TIME = 67584
NBLOCKS = 16
CHANNELS = 8192


def draw_records(key, part):
    noise_key, chan_key, time_key = jax.random.split(key, 3)
    window_count = TIME // (SEG_LEN // 2)
    noise_field = jax.random.normal(noise_key, (TIME, CHANNELS), jnp.float32)
    chan_scale = jnp.exp(jax.random.uniform(chan_key, (1, CHANNELS), jnp.float32, 0.0, math.log(10.0)))
    window_scale = jnp.exp(jax.random.uniform(time_key, (window_count,), jnp.float32, 0.0, math.log(10.0)))
    time_scale = jnp.repeat(window_scale, SEG_LEN // 2)[:, None]
    return (noise_field * chan_scale * time_scale).astype(jnp.bfloat16)


def draw_offsets(key, part):
    start_span = RECORD_DEV - SEG_LEN + 1
    values = jax.random.randint(key, (SEGMENTS,), 0, start_span, jnp.int32)
    chosen = jax.random.randint(jax.random.fold_in(key, 7), (2,), 0, SEGMENTS, jnp.int32)
    values = values.at[chosen[1]].set(0)
    values = values.at[chosen[0]].set(start_span - 1)
    return values


def draw_band_blocks(key, part):
    low_count = max(1, NBLOCKS // 2 - 2)
    narrow_block = jax.random.randint(jax.random.fold_in(key, 11), (), 0, low_count, jnp.int32)
    block_index = jnp.arange(NBLOCKS, dtype=jnp.int32)
    values = jnp.full((NBLOCKS,), BAND, jnp.int32)
    values = jnp.where(block_index == narrow_block, 0, values)
    values = jnp.where(block_index == narrow_block + 1, 1, values)
    return values.astype(jnp.int32)


def set_ends(result, own_key, smallest, largest):
    longest = result.shape.index(max(result.shape))
    spots = []
    for shift in (0, 1):
        where = [jax.random.randint(jax.random.fold_in(own_key, axis), (), 0, length) for axis, length in enumerate(result.shape)]
        where[longest] = (where[longest] + shift) % result.shape[longest]
        spots.append(tuple(where))
    return result.at[spots[0]].set(smallest).at[spots[1]].set(largest)


def setup_inputs(seed: int = 0) -> dict:
    keys = jax.random.split(jax.random.key(seed), 5)
    return {
        "records": draw_records(jax.random.fold_in(keys[4], 71), 0),
        "offsets": draw_offsets(jax.random.fold_in(keys[4], 71), 0),
        "dead_mask": set_ends((jax.random.randint(keys[2], (CHANNELS,), 0, 16) < 15).astype(jnp.int32), jax.random.fold_in(keys[2], 1), 0, 1),
        "band_blocks": draw_band_blocks(jax.random.fold_in(keys[4], 71), 0),
    }


EPS_POWER = 1e-06

def dft_table(seg_length, bin_count, first_bin):
    sample_index = jnp.arange(seg_length, dtype=jnp.int32)
    row_index = jnp.arange(2 * bin_count, dtype=jnp.int32)
    harmonic = row_index // 2 + first_bin
    phase_steps = harmonic[:, None] * sample_index[None, :] % seg_length
    phase_angle = 2.0 * jnp.pi / seg_length * phase_steps.astype(jnp.float32)
    hann_taper = 0.5 - 0.5 * jnp.cos(2.0 * jnp.pi / seg_length * sample_index.astype(jnp.float32))
    wave_rows = jnp.where((row_index % 2 == 0)[:, None], jnp.cos(phase_angle), -jnp.sin(phase_angle))
    return (hann_taper[None, :] * wave_rows).astype(jnp.bfloat16)

def reference(records, offsets, dead_mask, band_blocks):
    dft_rows = dft_table(SEG_LEN, BINS, FIRST_BIN)
    starts = jnp.arange(SEGMENTS, dtype=jnp.int32) // SEG_DEV * RECORD_DEV + offsets.astype(jnp.int32)
    live_mask = dead_mask.astype(jnp.float32)

    def one_segment(start_row):
        frame_rows = lax.dynamic_slice_in_dim(records, start_row, SEG_LEN, 0)
        spectra = jnp.dot(dft_rows, frame_rows, preferred_element_type=jnp.float32)
        band_power = lax.optimization_barrier(jnp.sum(spectra * spectra, axis=0)) * (1.0 / BINS)
        scaling = live_mask / jnp.sqrt(band_power + EPS_POWER)
        return (spectra * scaling[None, :]).astype(jnp.bfloat16)
    whitened = lax.map(one_segment, starts)
    panels = whitened.reshape(SEGMENTS, BINS, 2, CHANNELS).transpose(1, 2, 0, 3)
    panels = panels.reshape(BINS, 2 * SEGMENTS, NBLOCKS, CB)
    band_limit = band_blocks.astype(jnp.int32)

    def one_bin(bin_panel):
        left_panel = bin_panel.astype(jnp.float32)
        turned = jnp.concatenate([left_panel[SEGMENTS:], -left_panel[:SEGMENTS]], axis=0)
        outputs = []
        for offset_index in range(BAND + 1):
            right_panel = jnp.concatenate([left_panel[:, offset_index:], jnp.zeros((2 * SEGMENTS, offset_index, CB), jnp.float32)], axis=1)
            real_part = jnp.einsum('sbi,sbj->bij', left_panel, right_panel, precision=lax.Precision.HIGHEST)
            imag_part = jnp.einsum('sbi,sbj->bij', turned, right_panel, precision=lax.Precision.HIGHEST)
            cross_block = jnp.concatenate([real_part, imag_part], axis=2) * (1.0 / SEGMENTS)
            keep_flag = (offset_index <= band_limit).astype(jnp.bfloat16)
            outputs.append(cross_block.astype(jnp.bfloat16) * keep_flag[:, None, None])
        return jnp.stack(outputs, axis=0)
    per_bin = lax.map(one_bin, panels)
    return per_bin.transpose(1, 0, 2, 3, 4).reshape(BAND + 1, BINS, CHANNELS, 2 * CB)
```

```python
import jax
import jax.numpy as jnp
from jax import lax
from jax.sharding import PartitionSpec as P

SEG_LEN = 256
BINS = 32
FIRST_BIN = 2


EPS_POWER = 1e-06


def from_behind(block, axis, distance):
    devices = range(lax.axis_size(axis))
    route = [(i - distance, i) for i in devices if i - distance in devices]
    return lax.ppermute(block, axis, route)


def dft_table(seg_length, bin_count, first_bin):
    sample_index = jnp.arange(seg_length, dtype=jnp.int32)
    row_index = jnp.arange(2 * bin_count, dtype=jnp.int32)
    harmonic = row_index // 2 + first_bin
    phase_steps = harmonic[:, None] * sample_index[None, :] % seg_length
    phase_angle = 2.0 * jnp.pi / seg_length * phase_steps.astype(jnp.float32)
    hann_taper = 0.5 - 0.5 * jnp.cos(2.0 * jnp.pi / seg_length * sample_index.astype(jnp.float32))
    wave_rows = jnp.where(
        (row_index % 2 == 0)[:, None], jnp.cos(phase_angle), -jnp.sin(phase_angle)
    )
    return (hann_taper[None, :] * wave_rows).astype(jnp.bfloat16)


def local_products(left_panel, partner_panels):
    seg_count = left_panel.shape[2]
    results = []
    for right_panel in partner_panels:
        turned = jnp.stack([-right_panel[:, 1], right_panel[:, 0]], axis=1)
        both = jnp.concatenate([right_panel, turned], axis=3)
        product = jnp.einsum(
            "fpsi,fpsj->fij", left_panel, both, preferred_element_type=jnp.float32
        )
        results.append(product * (1.0 / seg_count))
    return results


def shards(records, offsets, dead_mask, band_blocks):
    dft_rows = dft_table(SEG_LEN, BINS, FIRST_BIN)
    frames = jax.vmap(lambda start: lax.dynamic_slice_in_dim(records, start, SEG_LEN, 0))(offsets)
    spectra = jnp.einsum("kt,stc->ksc", dft_rows, frames, preferred_element_type=jnp.float32)
    band_power = jnp.sum(spectra * spectra, axis=0) * (1.0 / BINS)
    scaling = dead_mask.astype(jnp.float32)[None, :] / jnp.sqrt(band_power + EPS_POWER)
    whitened = (spectra * scaling[None]).astype(jnp.bfloat16)
    whitened = whitened.reshape(BINS, 2, whitened.shape[1], whitened.shape[2])
    own_panel = lax.all_to_all(whitened, "freq", split_axis=0, concat_axis=2, tiled=True)
    upper_panel = from_behind(own_panel, "chan", -1)
    second_panel = from_behind(own_panel, "chan", -2)
    products = local_products(own_panel, [own_panel, upper_panel, second_panel])
    band_limit = band_blocks[0]
    results = []
    for offset_index, product in enumerate(products):
        keep_flag = (offset_index <= band_limit).astype(jnp.bfloat16)
        results.append(product.astype(jnp.bfloat16) * keep_flag)
    return jnp.stack(results, axis=0)


def solution(mesh):
    in_specs = (P("freq", "chan"), P("freq"), P("chan"), P("chan"))
    out_specs = P(None, "freq", "chan", None)
    return jax.shard_map(shards, mesh=mesh, in_specs=in_specs, out_specs=out_specs, check_vma=False)
```

```python
import functools

import jax
import jax.numpy as jnp
from jax import lax
from jax.experimental import pallas as pl
from jax.experimental.pallas import tpu as pltpu
from jax.sharding import PartitionSpec as P

SEG_LEN = 256
BINS = 32
FIRST_BIN = 2


EPS_POWER = 1e-06


def from_behind(block, axis, distance):
    devices = range(lax.axis_size(axis))
    route = [(i - distance, i) for i in devices if i - distance in devices]
    return lax.ppermute(block, axis, route)


def dft_table(seg_length, bin_count, first_bin):
    sample_index = jnp.arange(seg_length, dtype=jnp.int32)
    row_index = jnp.arange(2 * bin_count, dtype=jnp.int32)
    harmonic = row_index // 2 + first_bin
    phase_steps = harmonic[:, None] * sample_index[None, :] % seg_length
    phase_angle = 2.0 * jnp.pi / seg_length * phase_steps.astype(jnp.float32)
    hann_taper = 0.5 - 0.5 * jnp.cos(2.0 * jnp.pi / seg_length * sample_index.astype(jnp.float32))
    wave_rows = jnp.where(
        (row_index % 2 == 0)[:, None], jnp.cos(phase_angle), -jnp.sin(phase_angle)
    )
    return (hann_taper[None, :] * wave_rows).astype(jnp.bfloat16)


def spectra_kernel(seg_count, window, offs_ref, dft_ref, mask_ref, rec_hbm, out_ref, frames, sems):
    last_start = rec_hbm.shape[0] - window
    starts = []
    copies = []
    for j in range(seg_count):
        offset = offs_ref[j]
        start = pl.multiple_of(jnp.minimum((offset // 16) * 16, last_start), 16)
        starts.append(offset - start)
        copies.append(
            pltpu.make_async_copy(rec_hbm.at[pl.ds(start, window)], frames.at[j], sems.at[j])
        )
    for copy in copies:
        copy.start()
    dft = dft_ref[...]
    live = mask_ref[...]
    for j in range(seg_count):
        shifted = pltpu.roll(dft, starts[j], 1).astype(jnp.bfloat16)
        copies[j].wait()
        spec = jnp.dot(shifted, frames[j], preferred_element_type=jnp.float32)
        power = jnp.sum(spec * spec, axis=0, keepdims=True) * (1.0 / BINS)
        scale = live / jnp.sqrt(power + EPS_POWER)
        out_ref[j] = (spec * scale).astype(out_ref.dtype)


def whitened_spectra(records, offsets, dead_mask):
    seg_count = offsets.shape[0]
    channels = records.shape[1]
    window = SEG_LEN + 128
    dft_rows = dft_table(SEG_LEN, BINS, FIRST_BIN)
    rows = dft_rows.shape[0]
    padded = jnp.pad(dft_rows.astype(jnp.float32), ((0, 0), (0, window - SEG_LEN)))
    live = dead_mask.astype(jnp.float32).reshape(1, channels)
    return pl.pallas_call(
        functools.partial(spectra_kernel, seg_count, window),
        out_shape=jax.ShapeDtypeStruct((seg_count, rows, channels), jnp.bfloat16),
        grid_spec=pltpu.PrefetchScalarGridSpec(
            num_scalar_prefetch=1,
            grid=(1,),
            in_specs=[
                pl.BlockSpec((rows, window), lambda i, offs: (0, 0)),
                pl.BlockSpec((1, channels), lambda i, offs: (0, 0)),
                pl.BlockSpec(memory_space=pl.ANY),
            ],
            out_specs=pl.BlockSpec((seg_count, rows, channels), lambda i, offs: (0, 0, 0)),
            scratch_shapes=[
                pltpu.VMEM((seg_count, window, channels), records.dtype),
                pltpu.SemaphoreType.DMA((seg_count,)),
            ],
        ),
        compiler_params=pltpu.CompilerParams(vmem_limit_bytes=56 * 1024 * 1024),
        cost_estimate=pl.CostEstimate(
            flops=2 * seg_count * rows * window * channels,
            bytes_accessed=seg_count * (window + rows) * channels * 2,
            transcendentals=seg_count * channels,
        ),
    )(offsets, padded, live, records)


def local_products(left_panel, partner_panels):
    seg_count = left_panel.shape[2]
    results = []
    for right_panel in partner_panels:
        turned = jnp.stack([-right_panel[:, 1], right_panel[:, 0]], axis=1)
        both = jnp.concatenate([right_panel, turned], axis=3)
        product = jnp.einsum(
            "fpsi,fpsj->fij", left_panel, both, preferred_element_type=jnp.float32
        )
        results.append(product * (1.0 / seg_count))
    return results


def shards(records, offsets, dead_mask, band_blocks):
    per_segment = whitened_spectra(records, offsets, dead_mask)
    seg_count, rows, channels = per_segment.shape
    whitened = per_segment.reshape(seg_count, BINS, 2, channels).transpose(1, 2, 0, 3)
    own_panel = lax.all_to_all(whitened, "freq", split_axis=0, concat_axis=2, tiled=True)
    upper_panel = from_behind(own_panel, "chan", -1)
    second_panel = from_behind(own_panel, "chan", -2)
    products = local_products(own_panel, [own_panel, upper_panel, second_panel])
    band_limit = band_blocks[0]
    results = []
    for offset_index, product in enumerate(products):
        keep_flag = (offset_index <= band_limit).astype(jnp.bfloat16)
        results.append(product.astype(jnp.bfloat16) * keep_flag)
    return jnp.stack(results, axis=0)


def solution(mesh):
    in_specs = (P("freq", "chan"), P("freq"), P("chan"), P("chan"))
    out_specs = P(None, "freq", "chan", None)
    return jax.shard_map(shards, mesh=mesh, in_specs=in_specs, out_specs=out_specs, check_vma=False)
```

```python
import functools

import jax
import jax.numpy as jnp
from jax import lax
from jax.experimental import pallas as pl
from jax.experimental.pallas import tpu as pltpu
from jax.sharding import PartitionSpec as P

SEG_LEN = 256
BINS = 32
FIRST_BIN = 2
BAND = 2


EPS_POWER = 1e-06


def from_behind(block, axis, distance):
    devices = range(lax.axis_size(axis))
    route = [(i - distance, i) for i in devices if i - distance in devices]
    return lax.ppermute(block, axis, route)


def dft_table(seg_length, bin_count, first_bin):
    sample_index = jnp.arange(seg_length, dtype=jnp.int32)
    row_index = jnp.arange(2 * bin_count, dtype=jnp.int32)
    harmonic = row_index // 2 + first_bin
    phase_steps = harmonic[:, None] * sample_index[None, :] % seg_length
    phase_angle = 2.0 * jnp.pi / seg_length * phase_steps.astype(jnp.float32)
    hann_taper = 0.5 - 0.5 * jnp.cos(2.0 * jnp.pi / seg_length * sample_index.astype(jnp.float32))
    wave_rows = jnp.where(
        (row_index % 2 == 0)[:, None], jnp.cos(phase_angle), -jnp.sin(phase_angle)
    )
    return (hann_taper[None, :] * wave_rows).astype(jnp.bfloat16)


def spectra_kernel(seg_count, window, offs_ref, dft_ref, mask_ref, rec_hbm, out_ref, frames, sems):
    last_start = rec_hbm.shape[0] - window
    starts = []
    copies = []
    for j in range(seg_count):
        offset = offs_ref[j]
        start = pl.multiple_of(jnp.minimum((offset // 16) * 16, last_start), 16)
        starts.append(offset - start)
        copies.append(
            pltpu.make_async_copy(rec_hbm.at[pl.ds(start, window)], frames.at[j], sems.at[j])
        )
    for copy in copies:
        copy.start()
    dft = dft_ref[...]
    live = mask_ref[...]
    for j in range(seg_count):
        shifted = pltpu.roll(dft, starts[j], 1).astype(jnp.bfloat16)
        copies[j].wait()
        spec = jnp.dot(shifted, frames[j], preferred_element_type=jnp.float32)
        power = jnp.sum(spec * spec, axis=0, keepdims=True) * (1.0 / BINS)
        scale = live / jnp.sqrt(power + EPS_POWER)
        out_ref[j] = (spec * scale).astype(out_ref.dtype)


def whitened_spectra(records, offsets, dead_mask):
    seg_count = offsets.shape[0]
    channels = records.shape[1]
    window = SEG_LEN + 128
    dft_rows = dft_table(SEG_LEN, BINS, FIRST_BIN)
    rows = dft_rows.shape[0]
    padded = jnp.pad(dft_rows.astype(jnp.float32), ((0, 0), (0, window - SEG_LEN)))
    live = dead_mask.astype(jnp.float32).reshape(1, channels)
    return pl.pallas_call(
        functools.partial(spectra_kernel, seg_count, window),
        out_shape=jax.ShapeDtypeStruct((seg_count, rows, channels), jnp.bfloat16),
        grid_spec=pltpu.PrefetchScalarGridSpec(
            num_scalar_prefetch=1,
            grid=(1,),
            in_specs=[
                pl.BlockSpec((rows, window), lambda i, offs: (0, 0)),
                pl.BlockSpec((1, channels), lambda i, offs: (0, 0)),
                pl.BlockSpec(memory_space=pl.ANY),
            ],
            out_specs=pl.BlockSpec((seg_count, rows, channels), lambda i, offs: (0, 0, 0)),
            scratch_shapes=[
                pltpu.VMEM((seg_count, window, channels), records.dtype),
                pltpu.SemaphoreType.DMA((seg_count,)),
            ],
        ),
        compiler_params=pltpu.CompilerParams(vmem_limit_bytes=56 * 1024 * 1024),
        cost_estimate=pl.CostEstimate(
            flops=2 * seg_count * rows * window * channels,
            bytes_accessed=seg_count * (window + rows) * channels * 2,
            transcendentals=seg_count * channels,
        ),
    )(offsets, padded, live, records)


def local_products(left_panel, partner_panels):
    seg_count = left_panel.shape[2]
    results = []
    for right_panel in partner_panels:
        turned = jnp.stack([-right_panel[:, 1], right_panel[:, 0]], axis=1)
        both = jnp.concatenate([right_panel, turned], axis=3)
        product = jnp.einsum(
            "fpsi,fpsj->fij", left_panel, both, preferred_element_type=jnp.float32
        )
        results.append(product * (1.0 / seg_count))
    return results


def exchange_panels(whitened, offsets_kept):
    n_chan = lax.axis_size("chan")
    n_freq = lax.axis_size("freq")
    bins, parts, seg_count, channels = whitened.shape
    groups = whitened.reshape(n_freq, bins // n_freq, parts, seg_count, channels)
    me = lax.axis_index("freq")
    pieces = [lax.dynamic_index_in_dim(groups, me ^ g, 0, keepdims=False) for g in range(n_freq)]
    panels = []
    for d in range(offsets_kept):
        received = []
        for g in range(n_freq):
            if d == 0 and g == 0:
                received.append(pieces[0])
                continue
            pairs = [
                (c * n_freq + f, (c - d) * n_freq + (f ^ g))
                for c in range(d, n_chan)
                for f in range(n_freq)
            ]
            received.append(lax.ppermute(pieces[g], ("chan", "freq"), pairs))
        panels.append(jnp.concatenate(received, axis=2))
    return panels


def shards(records, offsets, dead_mask, band_blocks):
    per_segment = whitened_spectra(records, offsets, dead_mask)
    seg_count, rows, channels = per_segment.shape
    whitened = per_segment.reshape(seg_count, BINS, 2, channels).transpose(1, 2, 0, 3)
    panels = exchange_panels(whitened, BAND + 1)
    products = local_products(panels[0], panels)
    band_limit = band_blocks[0]
    results = []
    for offset_index, product in enumerate(products):
        keep_flag = (offset_index <= band_limit).astype(jnp.bfloat16)
        results.append(product.astype(jnp.bfloat16) * keep_flag)
    return jnp.stack(results, axis=0)


def solution(mesh):
    in_specs = (P("freq", "chan"), P("freq"), P("chan"), P("chan"))
    out_specs = P(None, "freq", "chan", None)
    return jax.shard_map(shards, mesh=mesh, in_specs=in_specs, out_specs=out_specs, check_vma=False)
```

```python
import functools

import jax
import jax.numpy as jnp
from jax import lax
from jax.experimental import pallas as pl
from jax.experimental.pallas import tpu as pltpu
from jax.sharding import PartitionSpec as P

SEG_LEN = 256
BINS = 32
FIRST_BIN = 2
BAND = 2


EPS_POWER = 1e-06


def from_behind(block, axis, distance):
    devices = range(lax.axis_size(axis))
    route = [(i - distance, i) for i in devices if i - distance in devices]
    return lax.ppermute(block, axis, route)


def dft_table(seg_length, bin_count, first_bin):
    sample_index = jnp.arange(seg_length, dtype=jnp.int32)
    row_index = jnp.arange(2 * bin_count, dtype=jnp.int32)
    harmonic = row_index // 2 + first_bin
    phase_steps = harmonic[:, None] * sample_index[None, :] % seg_length
    phase_angle = 2.0 * jnp.pi / seg_length * phase_steps.astype(jnp.float32)
    hann_taper = 0.5 - 0.5 * jnp.cos(2.0 * jnp.pi / seg_length * sample_index.astype(jnp.float32))
    wave_rows = jnp.where(
        (row_index % 2 == 0)[:, None], jnp.cos(phase_angle), -jnp.sin(phase_angle)
    )
    return (hann_taper[None, :] * wave_rows).astype(jnp.bfloat16)


def spectra_kernel(seg_count, window, offs_ref, dft_ref, mask_ref, rec_hbm, out_ref, frames, sems):
    last_start = rec_hbm.shape[0] - window
    starts = []
    copies = []
    for j in range(seg_count):
        offset = offs_ref[j]
        start = pl.multiple_of(jnp.minimum((offset // 16) * 16, last_start), 16)
        starts.append(offset - start)
        copies.append(
            pltpu.make_async_copy(rec_hbm.at[pl.ds(start, window)], frames.at[j], sems.at[j])
        )
    for copy in copies:
        copy.start()
    dft = dft_ref[...]
    live = mask_ref[...]
    for j in range(seg_count):
        shifted = pltpu.roll(dft, starts[j], 1).astype(jnp.bfloat16)
        copies[j].wait()
        spec = jnp.dot(shifted, frames[j], preferred_element_type=jnp.float32)
        power = jnp.sum(spec * spec, axis=0, keepdims=True) * (1.0 / BINS)
        scale = live / jnp.sqrt(power + EPS_POWER)
        out_ref[j] = (spec * scale).astype(out_ref.dtype)


def whitened_spectra(records, offsets, dead_mask):
    seg_count = offsets.shape[0]
    channels = records.shape[1]
    window = SEG_LEN + 128
    dft_rows = dft_table(SEG_LEN, BINS, FIRST_BIN)
    rows = dft_rows.shape[0]
    padded = jnp.pad(dft_rows.astype(jnp.float32), ((0, 0), (0, window - SEG_LEN)))
    live = dead_mask.astype(jnp.float32).reshape(1, channels)
    return pl.pallas_call(
        functools.partial(spectra_kernel, seg_count, window),
        out_shape=jax.ShapeDtypeStruct((seg_count, rows, channels), jnp.bfloat16),
        grid_spec=pltpu.PrefetchScalarGridSpec(
            num_scalar_prefetch=1,
            grid=(1,),
            in_specs=[
                pl.BlockSpec((rows, window), lambda i, offs: (0, 0)),
                pl.BlockSpec((1, channels), lambda i, offs: (0, 0)),
                pl.BlockSpec(memory_space=pl.ANY),
            ],
            out_specs=pl.BlockSpec((seg_count, rows, channels), lambda i, offs: (0, 0, 0)),
            scratch_shapes=[
                pltpu.VMEM((seg_count, window, channels), records.dtype),
                pltpu.SemaphoreType.DMA((seg_count,)),
            ],
        ),
        compiler_params=pltpu.CompilerParams(vmem_limit_bytes=56 * 1024 * 1024),
        cost_estimate=pl.CostEstimate(
            flops=2 * seg_count * rows * window * channels,
            bytes_accessed=seg_count * (window + rows) * channels * 2,
            transcendentals=seg_count * channels,
        ),
    )(offsets, padded, live, records)


def local_products(left_panel, partner_panels):
    seg_count = left_panel.shape[2]
    results = []
    for right_panel in partner_panels:
        turned = jnp.stack([-right_panel[:, 1], right_panel[:, 0]], axis=1)
        both = jnp.concatenate([right_panel, turned], axis=3)
        product = jnp.einsum(
            "fpsi,fpsj->fij", left_panel, both, preferred_element_type=jnp.float32
        )
        results.append(product * (1.0 / seg_count))
    return results


def neighbour_panels(own_panel):
    n_chan = lax.axis_size("chan")
    second_panel = from_behind(own_panel, "chan", -2)
    from_sibling = lax.ppermute(own_panel, "chan", [(c + 1, c) for c in range(0, n_chan, 2)])
    from_forward = lax.ppermute(second_panel, "chan", [(c - 1, c) for c in range(1, n_chan, 2)])
    odd = lax.axis_index("chan") % 2 == 1
    upper_panel = jnp.where(odd, from_forward, from_sibling)
    return upper_panel, second_panel


def shards(records, offsets, dead_mask, band_blocks):
    per_segment = whitened_spectra(records, offsets, dead_mask)
    seg_count, rows, channels = per_segment.shape
    whitened = per_segment.reshape(seg_count, BINS, 2, channels).transpose(1, 2, 0, 3)
    n_freq = lax.axis_size("freq")
    per_device = BINS // n_freq
    chunks = 2
    grouped = whitened.reshape(n_freq, chunks, per_device // chunks, 2, seg_count, channels)
    chunk_products = []
    for k in range(chunks):
        part = grouped[:, k].reshape(BINS // chunks, 2, seg_count, channels)
        own_panel = lax.all_to_all(part, "freq", split_axis=0, concat_axis=2, tiled=True)
        upper_panel, second_panel = neighbour_panels(own_panel)
        chunk_products.append(local_products(own_panel, [own_panel, upper_panel, second_panel]))
    band_limit = band_blocks[0]
    results = []
    for offset_index in range(BAND + 1):
        product = jnp.concatenate([p[offset_index] for p in chunk_products], axis=0)
        keep_flag = (offset_index <= band_limit).astype(jnp.bfloat16)
        results.append(product.astype(jnp.bfloat16) * keep_flag)
    return jnp.stack(results, axis=0)


def solution(mesh):
    in_specs = (P("freq", "chan"), P("freq"), P("chan"), P("chan"))
    out_specs = P(None, "freq", "chan", None)
    return jax.shard_map(shards, mesh=mesh, in_specs=in_specs, out_specs=out_specs, check_vma=False)
```

```python
import functools

import jax
import jax.numpy as jnp
from jax import lax
from jax.experimental import pallas as pl
from jax.experimental.pallas import tpu as pltpu
from jax.sharding import PartitionSpec as P

SEG_LEN = 256
BINS = 32
FIRST_BIN = 2
BAND = 2


EPS_POWER = 1e-06


def from_behind(block, axis, distance):
    devices = range(lax.axis_size(axis))
    route = [(i - distance, i) for i in devices if i - distance in devices]
    return lax.ppermute(block, axis, route)


def dft_table(seg_length, bin_count, first_bin):
    sample_index = jnp.arange(seg_length, dtype=jnp.int32)
    row_index = jnp.arange(2 * bin_count, dtype=jnp.int32)
    harmonic = row_index // 2 + first_bin
    phase_steps = harmonic[:, None] * sample_index[None, :] % seg_length
    phase_angle = 2.0 * jnp.pi / seg_length * phase_steps.astype(jnp.float32)
    hann_taper = 0.5 - 0.5 * jnp.cos(2.0 * jnp.pi / seg_length * sample_index.astype(jnp.float32))
    wave_rows = jnp.where(
        (row_index % 2 == 0)[:, None], jnp.cos(phase_angle), -jnp.sin(phase_angle)
    )
    return (hann_taper[None, :] * wave_rows).astype(jnp.bfloat16)


def spectra_kernel(seg_count, window, offs_ref, dft_ref, mask_ref, rec_hbm, out_ref, frames, sems):
    last_start = rec_hbm.shape[0] - window
    starts = []
    copies = []
    for j in range(seg_count):
        offset = offs_ref[j]
        start = pl.multiple_of(jnp.minimum((offset // 16) * 16, last_start), 16)
        starts.append(offset - start)
        copies.append(
            pltpu.make_async_copy(rec_hbm.at[pl.ds(start, window)], frames.at[j], sems.at[j])
        )
    for copy in copies:
        copy.start()
    dft = dft_ref[...]
    live = mask_ref[...]
    for j in range(seg_count):
        shifted = pltpu.roll(dft, starts[j], 1).astype(jnp.bfloat16)
        copies[j].wait()
        spec = jnp.dot(shifted, frames[j], preferred_element_type=jnp.float32)
        power = jnp.sum(spec * spec, axis=0, keepdims=True) * (1.0 / BINS)
        scale = live / jnp.sqrt(power + EPS_POWER)
        out_ref[j] = (spec * scale).astype(out_ref.dtype)


def whitened_spectra(records, offsets, dead_mask):
    seg_count = offsets.shape[0]
    channels = records.shape[1]
    window = SEG_LEN + 128
    dft_rows = dft_table(SEG_LEN, BINS, FIRST_BIN)
    rows = dft_rows.shape[0]
    padded = jnp.pad(dft_rows.astype(jnp.float32), ((0, 0), (0, window - SEG_LEN)))
    live = dead_mask.astype(jnp.float32).reshape(1, channels)
    return pl.pallas_call(
        functools.partial(spectra_kernel, seg_count, window),
        out_shape=jax.ShapeDtypeStruct((seg_count, rows, channels), jnp.bfloat16),
        grid_spec=pltpu.PrefetchScalarGridSpec(
            num_scalar_prefetch=1,
            grid=(1,),
            in_specs=[
                pl.BlockSpec((rows, window), lambda i, offs: (0, 0)),
                pl.BlockSpec((1, channels), lambda i, offs: (0, 0)),
                pl.BlockSpec(memory_space=pl.ANY),
            ],
            out_specs=pl.BlockSpec((seg_count, rows, channels), lambda i, offs: (0, 0, 0)),
            scratch_shapes=[
                pltpu.VMEM((seg_count, window, channels), records.dtype),
                pltpu.SemaphoreType.DMA((seg_count,)),
            ],
        ),
        compiler_params=pltpu.CompilerParams(vmem_limit_bytes=56 * 1024 * 1024),
        cost_estimate=pl.CostEstimate(
            flops=2 * seg_count * rows * window * channels,
            bytes_accessed=seg_count * (window + rows) * channels * 2,
            transcendentals=seg_count * channels,
        ),
    )(offsets, padded, live, records)


def local_products(left_panel, partner_panels):
    seg_count = left_panel.shape[2]
    results = []
    for right_panel in partner_panels:
        turned = jnp.stack([-right_panel[:, 1], right_panel[:, 0]], axis=1)
        both = jnp.concatenate([right_panel, turned], axis=3)
        product = jnp.einsum(
            "fpsi,fpsj->fij", left_panel, both, preferred_element_type=jnp.float32
        )
        results.append(product * (1.0 / seg_count))
    return results


def neighbour_panels(own_panel):
    n_chan = lax.axis_size("chan")
    second_panel = from_behind(own_panel, "chan", -2)
    from_sibling = lax.ppermute(own_panel, "chan", [(c + 1, c) for c in range(0, n_chan, 2)])
    from_forward = lax.ppermute(second_panel, "chan", [(c - 1, c) for c in range(1, n_chan, 2)])
    odd = lax.axis_index("chan") % 2 == 1
    upper_panel = jnp.where(odd, from_forward, from_sibling)
    return upper_panel, second_panel


def shards(records, offsets, dead_mask, band_blocks):
    per_segment = whitened_spectra(records, offsets, dead_mask)
    seg_count, rows, channels = per_segment.shape
    whitened = per_segment.reshape(seg_count, BINS, 2, channels).transpose(1, 2, 0, 3)
    n_freq = lax.axis_size("freq")
    per_device = BINS // n_freq
    chunks = 4
    grouped = whitened.reshape(n_freq, chunks, per_device // chunks, 2, seg_count, channels)
    chunk_products = []
    for k in range(chunks):
        part = grouped[:, k].reshape(BINS // chunks, 2, seg_count, channels)
        own_panel = lax.all_to_all(part, "freq", split_axis=0, concat_axis=2, tiled=True)
        upper_panel, second_panel = neighbour_panels(own_panel)
        chunk_products.append(local_products(own_panel, [own_panel, upper_panel, second_panel]))
    band_limit = band_blocks[0]
    results = []
    for offset_index in range(BAND + 1):
        product = jnp.concatenate([p[offset_index] for p in chunk_products], axis=0)
        keep_flag = (offset_index <= band_limit).astype(jnp.bfloat16)
        results.append(product.astype(jnp.bfloat16) * keep_flag)
    return jnp.stack(results, axis=0)


def solution(mesh):
    in_specs = (P("freq", "chan"), P("freq"), P("chan"), P("chan"))
    out_specs = P(None, "freq", "chan", None)
    return jax.shard_map(shards, mesh=mesh, in_specs=in_specs, out_specs=out_specs, check_vma=False)
```

```python
import functools

import jax
import jax.numpy as jnp
from jax import lax
from jax.experimental import pallas as pl
from jax.experimental.pallas import tpu as pltpu
from jax.sharding import PartitionSpec as P

SEG_LEN = 256
BINS = 32
FIRST_BIN = 2
BAND = 2


EPS_POWER = 1e-06


def from_behind(block, axis, distance):
    devices = range(lax.axis_size(axis))
    route = [(i - distance, i) for i in devices if i - distance in devices]
    return lax.ppermute(block, axis, route)


def dft_table(seg_length, bin_count, first_bin):
    sample_index = jnp.arange(seg_length, dtype=jnp.int32)
    row_index = jnp.arange(2 * bin_count, dtype=jnp.int32)
    harmonic = row_index // 2 + first_bin
    phase_steps = harmonic[:, None] * sample_index[None, :] % seg_length
    phase_angle = 2.0 * jnp.pi / seg_length * phase_steps.astype(jnp.float32)
    hann_taper = 0.5 - 0.5 * jnp.cos(2.0 * jnp.pi / seg_length * sample_index.astype(jnp.float32))
    wave_rows = jnp.where(
        (row_index % 2 == 0)[:, None], jnp.cos(phase_angle), -jnp.sin(phase_angle)
    )
    return (hann_taper[None, :] * wave_rows).astype(jnp.bfloat16)


def spectra_kernel(seg_count, window, offs_ref, dft_ref, mask_ref, rec_hbm, out_ref, frames, sems):
    last_start = rec_hbm.shape[0] - window
    starts = []
    copies = []
    for j in range(seg_count):
        offset = offs_ref[j]
        start = pl.multiple_of(jnp.minimum((offset // 16) * 16, last_start), 16)
        starts.append(offset - start)
        copies.append(
            pltpu.make_async_copy(rec_hbm.at[pl.ds(start, window)], frames.at[j], sems.at[j])
        )
    for copy in copies:
        copy.start()
    dft = dft_ref[...]
    live = mask_ref[...]
    for j in range(seg_count):
        shifted = pltpu.roll(dft, starts[j], 1).astype(jnp.bfloat16)
        copies[j].wait()
        spec = jnp.dot(shifted, frames[j], preferred_element_type=jnp.float32)
        power = jnp.sum(spec * spec, axis=0, keepdims=True) * (1.0 / BINS)
        scale = live / jnp.sqrt(power + EPS_POWER)
        out_ref[j] = (spec * scale).astype(out_ref.dtype)


def whitened_spectra(records, offsets, dead_mask):
    seg_count = offsets.shape[0]
    channels = records.shape[1]
    window = SEG_LEN + 128
    dft_rows = dft_table(SEG_LEN, BINS, FIRST_BIN)
    rows = dft_rows.shape[0]
    padded = jnp.pad(dft_rows.astype(jnp.float32), ((0, 0), (0, window - SEG_LEN)))
    live = dead_mask.astype(jnp.float32).reshape(1, channels)
    return pl.pallas_call(
        functools.partial(spectra_kernel, seg_count, window),
        out_shape=jax.ShapeDtypeStruct((seg_count, rows, channels), jnp.bfloat16),
        grid_spec=pltpu.PrefetchScalarGridSpec(
            num_scalar_prefetch=1,
            grid=(1,),
            in_specs=[
                pl.BlockSpec((rows, window), lambda i, offs: (0, 0)),
                pl.BlockSpec((1, channels), lambda i, offs: (0, 0)),
                pl.BlockSpec(memory_space=pl.ANY),
            ],
            out_specs=pl.BlockSpec((seg_count, rows, channels), lambda i, offs: (0, 0, 0)),
            scratch_shapes=[
                pltpu.VMEM((seg_count, window, channels), records.dtype),
                pltpu.SemaphoreType.DMA((seg_count,)),
            ],
        ),
        compiler_params=pltpu.CompilerParams(vmem_limit_bytes=56 * 1024 * 1024),
        cost_estimate=pl.CostEstimate(
            flops=2 * seg_count * rows * window * channels,
            bytes_accessed=seg_count * (window + rows) * channels * 2,
            transcendentals=seg_count * channels,
        ),
    )(offsets, padded, live, records)


def local_products(left_panel, partner_panels):
    seg_count = left_panel.shape[2]
    results = []
    for right_panel in partner_panels:
        turned = jnp.stack([-right_panel[:, 1], right_panel[:, 0]], axis=1)
        both = jnp.concatenate([right_panel, turned], axis=3)
        product = jnp.einsum(
            "fpsi,fpsj->fij", left_panel, both, preferred_element_type=jnp.float32
        )
        results.append(product * (1.0 / seg_count))
    return results


def neighbour_panels(own_panel):
    n_chan = lax.axis_size("chan")
    second_panel = from_behind(own_panel, "chan", -2)
    from_sibling = lax.ppermute(own_panel, "chan", [(c + 1, c) for c in range(0, n_chan, 2)])
    from_forward = lax.ppermute(second_panel, "chan", [(c - 1, c) for c in range(1, n_chan, 2)])
    odd = lax.axis_index("chan") % 2 == 1
    upper_panel = jnp.where(odd, from_forward, from_sibling)
    return upper_panel, second_panel, from_sibling


def shards(records, offsets, dead_mask, band_blocks):
    per_segment = whitened_spectra(records, offsets, dead_mask)
    seg_count, rows, channels = per_segment.shape
    whitened = per_segment.reshape(seg_count, BINS, 2, channels).transpose(1, 2, 0, 3)
    n_freq = lax.axis_size("freq")
    per_device = BINS // n_freq
    chunks = 4
    grouped = whitened.reshape(n_freq, chunks, per_device // chunks, 2, seg_count, channels)
    parts = [grouped[:, k].reshape(BINS // chunks, 2, seg_count, channels) for k in range(chunks)]
    chunk_products = []
    for k in range(chunks):
        own_panel = lax.all_to_all(parts[k], "freq", split_axis=0, concat_axis=2, tiled=True)
        upper_panel, second_panel, from_sibling = neighbour_panels(own_panel)
        if k + 1 < chunks:
            _, parts[k + 1] = lax.optimization_barrier((from_sibling, parts[k + 1]))
        chunk_products.append(local_products(own_panel, [own_panel, upper_panel, second_panel]))
    band_limit = band_blocks[0]
    results = []
    for offset_index in range(BAND + 1):
        product = jnp.concatenate([p[offset_index] for p in chunk_products], axis=0)
        keep_flag = (offset_index <= band_limit).astype(jnp.bfloat16)
        results.append(product.astype(jnp.bfloat16) * keep_flag)
    return jnp.stack(results, axis=0)


def solution(mesh):
    in_specs = (P("freq", "chan"), P("freq"), P("chan"), P("chan"))
    out_specs = P(None, "freq", "chan", None)
    return jax.shard_map(shards, mesh=mesh, in_specs=in_specs, out_specs=out_specs, check_vma=False)
```

```python
import functools

import jax
import jax.numpy as jnp
from jax import lax
from jax.experimental import pallas as pl
from jax.experimental.pallas import tpu as pltpu
from jax.sharding import PartitionSpec as P

SEG_LEN = 256
BINS = 32
FIRST_BIN = 2
BAND = 2


EPS_POWER = 1e-06


def from_behind(block, axis, distance):
    devices = range(lax.axis_size(axis))
    route = [(i - distance, i) for i in devices if i - distance in devices]
    return lax.ppermute(block, axis, route)


def dft_table(seg_length, bin_count, first_bin):
    sample_index = jnp.arange(seg_length, dtype=jnp.int32)
    row_index = jnp.arange(2 * bin_count, dtype=jnp.int32)
    harmonic = row_index // 2 + first_bin
    phase_steps = harmonic[:, None] * sample_index[None, :] % seg_length
    phase_angle = 2.0 * jnp.pi / seg_length * phase_steps.astype(jnp.float32)
    hann_taper = 0.5 - 0.5 * jnp.cos(2.0 * jnp.pi / seg_length * sample_index.astype(jnp.float32))
    wave_rows = jnp.where(
        (row_index % 2 == 0)[:, None], jnp.cos(phase_angle), -jnp.sin(phase_angle)
    )
    return (hann_taper[None, :] * wave_rows).astype(jnp.bfloat16)


def spectra_kernel(seg_count, window, offs_ref, dft_ref, mask_ref, rec_hbm, out_ref, frames, sems):
    last_start = rec_hbm.shape[0] - window
    starts = []
    copies = []
    for j in range(seg_count):
        offset = offs_ref[j]
        start = pl.multiple_of(jnp.minimum((offset // 16) * 16, last_start), 16)
        starts.append(offset - start)
        copies.append(
            pltpu.make_async_copy(rec_hbm.at[pl.ds(start, window)], frames.at[j], sems.at[j])
        )
    for copy in copies:
        copy.start()
    dft = dft_ref[...]
    live = mask_ref[...]
    for j in range(seg_count):
        shifted = pltpu.roll(dft, starts[j], 1).astype(jnp.bfloat16)
        copies[j].wait()
        spec = jnp.dot(shifted, frames[j], preferred_element_type=jnp.float32)
        power = jnp.sum(spec * spec, axis=0, keepdims=True) * (1.0 / BINS)
        scale = live / jnp.sqrt(power + EPS_POWER)
        out_ref[j] = (spec * scale).astype(out_ref.dtype)


def whitened_spectra(records, offsets, dead_mask):
    seg_count = offsets.shape[0]
    channels = records.shape[1]
    window = SEG_LEN + 128
    dft_rows = dft_table(SEG_LEN, BINS, FIRST_BIN)
    rows = dft_rows.shape[0]
    padded = jnp.pad(dft_rows.astype(jnp.float32), ((0, 0), (0, window - SEG_LEN)))
    live = dead_mask.astype(jnp.float32).reshape(1, channels)
    return pl.pallas_call(
        functools.partial(spectra_kernel, seg_count, window),
        out_shape=jax.ShapeDtypeStruct((seg_count, rows, channels), jnp.bfloat16),
        grid_spec=pltpu.PrefetchScalarGridSpec(
            num_scalar_prefetch=1,
            grid=(1,),
            in_specs=[
                pl.BlockSpec((rows, window), lambda i, offs: (0, 0)),
                pl.BlockSpec((1, channels), lambda i, offs: (0, 0)),
                pl.BlockSpec(memory_space=pl.ANY),
            ],
            out_specs=pl.BlockSpec((seg_count, rows, channels), lambda i, offs: (0, 0, 0)),
            scratch_shapes=[
                pltpu.VMEM((seg_count, window, channels), records.dtype),
                pltpu.SemaphoreType.DMA((seg_count,)),
            ],
        ),
        compiler_params=pltpu.CompilerParams(vmem_limit_bytes=56 * 1024 * 1024),
        cost_estimate=pl.CostEstimate(
            flops=2 * seg_count * rows * window * channels,
            bytes_accessed=seg_count * (window + rows) * channels * 2,
            transcendentals=seg_count * channels,
        ),
    )(offsets, padded, live, records)


def local_products(left_panel, partner_panels):
    seg_count = left_panel.shape[2]
    results = []
    for right_panel in partner_panels:
        turned = jnp.stack([-right_panel[:, 1], right_panel[:, 0]], axis=1)
        both = jnp.concatenate([right_panel, turned], axis=3)
        product = jnp.einsum(
            "fpsi,fpsj->fij", left_panel, both, preferred_element_type=jnp.float32
        )
        results.append(product * (1.0 / seg_count))
    return results


def block_slice(panel, start, size):
    return lax.dynamic_slice_in_dim(panel, start, size, axis=2)


def chunk_exchange(part, seg_count):
    n_chan = lax.axis_size("chan")
    n_freq = lax.axis_size("freq")
    half = n_freq // 2
    me = lax.axis_index("freq")
    side = me // half
    row = me % half
    crossed = []
    for gy in range(half):
        g = half + gy
        piece = lax.dynamic_index_in_dim(part, me ^ g, 0, keepdims=False)
        pairs = [
            (c * n_freq + f, (c - 2) * n_freq + (f ^ g)) for c in range(2, n_chan) for f in range(n_freq)
        ]
        crossed.append(lax.ppermute(piece, ("chan", "freq"), pairs))
    flat = part.reshape((n_freq * part.shape[1],) + part.shape[2:])
    own_panel = lax.all_to_all(flat, "freq", split_axis=0, concat_axis=2, tiled=True)
    near = half * seg_count
    near_own = block_slice(own_panel, side * near, near)
    near_second = from_behind(near_own, "chan", -2)
    second_panel = jnp.concatenate([near_second] + crossed, axis=2)
    far_own = [
        block_slice(own_panel, (half * (1 - side) + (row ^ gy)) * seg_count, seg_count)
        for gy in range(half)
    ]
    second_left = jnp.concatenate([near_own] + far_own, axis=2)
    from_sibling = lax.ppermute(own_panel, "chan", [(c + 1, c) for c in range(0, n_chan, 2)])
    from_forward = lax.ppermute(second_panel, "chan", [(c - 1, c) for c in range(1, n_chan, 2)])
    odd = lax.axis_index("chan") % 2 == 1
    upper_panel = jnp.where(odd, from_forward, from_sibling)
    upper_left = jnp.where(odd, second_left, own_panel)
    return [own_panel, upper_left, second_left], [own_panel, upper_panel, second_panel]


def products_of(lefts, rights):
    seg_count = lefts[0].shape[2]
    results = []
    for left_panel, right_panel in zip(lefts, rights):
        turned = jnp.stack([-right_panel[:, 1], right_panel[:, 0]], axis=1)
        both = jnp.concatenate([right_panel, turned], axis=3)
        product = jnp.einsum(
            "fpsi,fpsj->fij", left_panel, both, preferred_element_type=jnp.float32
        )
        results.append(product * (1.0 / seg_count))
    return results


def shards(records, offsets, dead_mask, band_blocks):
    per_segment = whitened_spectra(records, offsets, dead_mask)
    seg_count, rows, channels = per_segment.shape
    whitened = per_segment.reshape(seg_count, BINS, 2, channels).transpose(1, 2, 0, 3)
    n_freq = lax.axis_size("freq")
    per_device = BINS // n_freq
    chunks = 1
    grouped = whitened.reshape(n_freq, chunks, per_device // chunks, 2, seg_count, channels)
    chunk_products = []
    for k in range(chunks):
        lefts, rights = chunk_exchange(grouped[:, k], seg_count)
        chunk_products.append(products_of(lefts, rights))
    band_limit = band_blocks[0]
    results = []
    for offset_index in range(BAND + 1):
        product = jnp.concatenate([p[offset_index] for p in chunk_products], axis=0)
        keep_flag = (offset_index <= band_limit).astype(jnp.bfloat16)
        results.append(product.astype(jnp.bfloat16) * keep_flag)
    return jnp.stack(results, axis=0)


def solution(mesh):
    in_specs = (P("freq", "chan"), P("freq"), P("chan"), P("chan"))
    out_specs = P(None, "freq", "chan", None)
    return jax.shard_map(shards, mesh=mesh, in_specs=in_specs, out_specs=out_specs, check_vma=False)
```

```python
import functools

import jax
import jax.numpy as jnp
from jax import lax
from jax.experimental import pallas as pl
from jax.experimental.pallas import tpu as pltpu
from jax.sharding import PartitionSpec as P

SEG_LEN = 256
BINS = 32
FIRST_BIN = 2
BAND = 2


EPS_POWER = 1e-06


def from_behind(block, axis, distance):
    devices = range(lax.axis_size(axis))
    route = [(i - distance, i) for i in devices if i - distance in devices]
    return lax.ppermute(block, axis, route)


def dft_table(seg_length, bin_count, first_bin):
    sample_index = jnp.arange(seg_length, dtype=jnp.int32)
    row_index = jnp.arange(2 * bin_count, dtype=jnp.int32)
    harmonic = row_index // 2 + first_bin
    phase_steps = harmonic[:, None] * sample_index[None, :] % seg_length
    phase_angle = 2.0 * jnp.pi / seg_length * phase_steps.astype(jnp.float32)
    hann_taper = 0.5 - 0.5 * jnp.cos(2.0 * jnp.pi / seg_length * sample_index.astype(jnp.float32))
    wave_rows = jnp.where(
        (row_index % 2 == 0)[:, None], jnp.cos(phase_angle), -jnp.sin(phase_angle)
    )
    return (hann_taper[None, :] * wave_rows).astype(jnp.bfloat16)


def spectra_kernel(seg_count, window, offs_ref, dft_ref, mask_ref, rec_hbm, out_ref, frames, sems):
    last_start = rec_hbm.shape[0] - window
    starts = []
    copies = []
    for j in range(seg_count):
        offset = offs_ref[j]
        start = pl.multiple_of(jnp.minimum((offset // 16) * 16, last_start), 16)
        starts.append(offset - start)
        copies.append(
            pltpu.make_async_copy(rec_hbm.at[pl.ds(start, window)], frames.at[j], sems.at[j])
        )
    for copy in copies:
        copy.start()
    dft = dft_ref[...]
    live = mask_ref[...]
    for j in range(seg_count):
        shifted = pltpu.roll(dft, starts[j], 1).astype(jnp.bfloat16)
        copies[j].wait()
        spec = jnp.dot(shifted, frames[j], preferred_element_type=jnp.float32)
        power = jnp.sum(spec * spec, axis=0, keepdims=True) * (1.0 / BINS)
        scale = live / jnp.sqrt(power + EPS_POWER)
        out_ref[j] = (spec * scale).astype(out_ref.dtype)


def whitened_spectra(records, offsets, dead_mask):
    seg_count = offsets.shape[0]
    channels = records.shape[1]
    window = SEG_LEN + 128
    dft_rows = dft_table(SEG_LEN, BINS, FIRST_BIN)
    rows = dft_rows.shape[0]
    padded = jnp.pad(dft_rows.astype(jnp.float32), ((0, 0), (0, window - SEG_LEN)))
    live = dead_mask.astype(jnp.float32).reshape(1, channels)
    return pl.pallas_call(
        functools.partial(spectra_kernel, seg_count, window),
        out_shape=jax.ShapeDtypeStruct((seg_count, rows, channels), jnp.bfloat16),
        grid_spec=pltpu.PrefetchScalarGridSpec(
            num_scalar_prefetch=1,
            grid=(1,),
            in_specs=[
                pl.BlockSpec((rows, window), lambda i, offs: (0, 0)),
                pl.BlockSpec((1, channels), lambda i, offs: (0, 0)),
                pl.BlockSpec(memory_space=pl.ANY),
            ],
            out_specs=pl.BlockSpec((seg_count, rows, channels), lambda i, offs: (0, 0, 0)),
            scratch_shapes=[
                pltpu.VMEM((seg_count, window, channels), records.dtype),
                pltpu.SemaphoreType.DMA((seg_count,)),
            ],
        ),
        compiler_params=pltpu.CompilerParams(vmem_limit_bytes=56 * 1024 * 1024),
        cost_estimate=pl.CostEstimate(
            flops=2 * seg_count * rows * window * channels,
            bytes_accessed=seg_count * (window + rows) * channels * 2,
            transcendentals=seg_count * channels,
        ),
    )(offsets, padded, live, records)


def local_products(left_panel, partner_panels):
    seg_count = left_panel.shape[2]
    results = []
    for right_panel in partner_panels:
        turned = jnp.stack([-right_panel[:, 1], right_panel[:, 0]], axis=1)
        both = jnp.concatenate([right_panel, turned], axis=3)
        product = jnp.einsum(
            "fpsi,fpsj->fij", left_panel, both, preferred_element_type=jnp.float32
        )
        results.append(product * (1.0 / seg_count))
    return results


def block_slice(panel, start, size):
    return lax.dynamic_slice_in_dim(panel, start, size, axis=2)


def chunk_exchange(part, seg_count):
    n_chan = lax.axis_size("chan")
    n_freq = lax.axis_size("freq")
    half = n_freq // 2
    me = lax.axis_index("freq")
    side = me // half
    row = me % half
    pieces = [lax.dynamic_index_in_dim(part, me ^ (half + gy), 0, keepdims=False) for gy in range(half)]
    flat = part.reshape((n_freq * part.shape[1],) + part.shape[2:])
    *pieces, flat = lax.optimization_barrier((*pieces, flat))
    crossed = []
    for gy in range(half):
        g = half + gy
        pairs = [
            (c * n_freq + f, (c - 2) * n_freq + (f ^ g)) for c in range(2, n_chan) for f in range(n_freq)
        ]
        crossed.append(lax.ppermute(pieces[gy], ("chan", "freq"), pairs))
    own_panel = lax.all_to_all(flat, "freq", split_axis=0, concat_axis=2, tiled=True)
    near = half * seg_count
    near_own = block_slice(own_panel, side * near, near)
    chan_me = lax.axis_index("chan")
    second_chip = (chan_me // 2) % 2 == 1
    down_z = lax.ppermute(near_own, "chan", [(c, c - 4) for c in range(4, n_chan) if (c // 2) % 2 == 0])
    outgoing = jnp.where(second_chip, near_own, down_z)
    across = [(c, c - 2) for c in range(n_chan) if (c // 2) % 2 == 1]
    across += [(c, c + 2) for c in range(n_chan - 4) if (c // 2) % 2 == 0]
    near_second = lax.ppermute(outgoing, "chan", across)
    second_panel = jnp.concatenate([near_second] + crossed, axis=2)
    far_own = [
        block_slice(own_panel, (half * (1 - side) + (row ^ gy)) * seg_count, seg_count)
        for gy in range(half)
    ]
    second_left = jnp.concatenate([near_own] + far_own, axis=2)
    from_sibling = lax.ppermute(own_panel, "chan", [(c + 1, c) for c in range(0, n_chan, 2)])
    from_forward = lax.ppermute(second_panel, "chan", [(c - 1, c) for c in range(1, n_chan, 2)])
    odd = lax.axis_index("chan") % 2 == 1
    upper_panel = jnp.where(odd, from_forward, from_sibling)
    upper_left = jnp.where(odd, second_left, own_panel)
    return [own_panel, upper_left, second_left], [own_panel, upper_panel, second_panel], from_sibling


def products_of(lefts, rights):
    seg_count = lefts[0].shape[2]
    results = []
    for left_panel, right_panel in zip(lefts, rights):
        turned = jnp.stack([-right_panel[:, 1], right_panel[:, 0]], axis=1)
        both = jnp.concatenate([right_panel, turned], axis=3)
        product = jnp.einsum(
            "fpsi,fpsj->fij", left_panel, both, preferred_element_type=jnp.float32
        )
        results.append(product * (1.0 / seg_count))
    return results


def shards(records, offsets, dead_mask, band_blocks):
    per_segment = whitened_spectra(records, offsets, dead_mask)
    seg_count, rows, channels = per_segment.shape
    whitened = per_segment.reshape(seg_count, BINS, 2, channels).transpose(1, 2, 0, 3)
    n_freq = lax.axis_size("freq")
    per_device = BINS // n_freq
    chunks = 2
    grouped = whitened.reshape(n_freq, chunks, per_device // chunks, 2, seg_count, channels)
    chunk_products = []
    parts = [grouped[:, k] for k in range(chunks)]
    for k in range(chunks):
        lefts, rights, from_sibling = chunk_exchange(parts[k], seg_count)
        if k + 1 < chunks:
            _, parts[k + 1] = lax.optimization_barrier((from_sibling, parts[k + 1]))
        chunk_products.append(products_of(lefts, rights))
    band_limit = band_blocks[0]
    results = []
    for offset_index in range(BAND + 1):
        product = jnp.concatenate([p[offset_index] for p in chunk_products], axis=0)
        keep_flag = (offset_index <= band_limit).astype(jnp.bfloat16)
        results.append(product.astype(jnp.bfloat16) * keep_flag)
    return jnp.stack(results, axis=0)


def solution(mesh):
    in_specs = (P("freq", "chan"), P("freq"), P("chan"), P("chan"))
    out_specs = P(None, "freq", "chan", None)
    return jax.shard_map(shards, mesh=mesh, in_specs=in_specs, out_specs=out_specs, check_vma=False)
```

```python
import functools

import jax
import jax.numpy as jnp
from jax import lax
from jax.experimental import pallas as pl
from jax.experimental.pallas import tpu as pltpu
from jax.sharding import PartitionSpec as P

SEG_LEN = 256
BINS = 32
FIRST_BIN = 2
BAND = 2


EPS_POWER = 1e-06


def from_behind(block, axis, distance):
    devices = range(lax.axis_size(axis))
    route = [(i - distance, i) for i in devices if i - distance in devices]
    return lax.ppermute(block, axis, route)


def dft_table(seg_length, bin_count, first_bin):
    sample_index = jnp.arange(seg_length, dtype=jnp.int32)
    row_index = jnp.arange(2 * bin_count, dtype=jnp.int32)
    harmonic = row_index // 2 + first_bin
    phase_steps = harmonic[:, None] * sample_index[None, :] % seg_length
    phase_angle = 2.0 * jnp.pi / seg_length * phase_steps.astype(jnp.float32)
    hann_taper = 0.5 - 0.5 * jnp.cos(2.0 * jnp.pi / seg_length * sample_index.astype(jnp.float32))
    wave_rows = jnp.where(
        (row_index % 2 == 0)[:, None], jnp.cos(phase_angle), -jnp.sin(phase_angle)
    )
    return (hann_taper[None, :] * wave_rows).astype(jnp.bfloat16)


def spectra_kernel(seg_count, window, offs_ref, dft_ref, mask_ref, rec_hbm, out_ref, frames, sems):
    last_start = rec_hbm.shape[0] - window
    starts = []
    copies = []
    for j in range(seg_count):
        offset = offs_ref[j]
        start = pl.multiple_of(jnp.minimum((offset // 16) * 16, last_start), 16)
        starts.append(offset - start)
        copies.append(
            pltpu.make_async_copy(rec_hbm.at[pl.ds(start, window)], frames.at[j], sems.at[j])
        )
    for copy in copies:
        copy.start()
    dft = dft_ref[...]
    live = mask_ref[...]
    for j in range(seg_count):
        shifted = pltpu.roll(dft, starts[j], 1).astype(jnp.bfloat16)
        copies[j].wait()
        spec = jnp.dot(shifted, frames[j], preferred_element_type=jnp.float32)
        power = jnp.sum(spec * spec, axis=0, keepdims=True) * (1.0 / BINS)
        scale = live / jnp.sqrt(power + EPS_POWER)
        out_ref[j] = (spec * scale).astype(out_ref.dtype)


def whitened_spectra(records, offsets, dead_mask):
    seg_count = offsets.shape[0]
    channels = records.shape[1]
    window = SEG_LEN + 128
    dft_rows = dft_table(SEG_LEN, BINS, FIRST_BIN)
    rows = dft_rows.shape[0]
    padded = jnp.pad(dft_rows.astype(jnp.float32), ((0, 0), (0, window - SEG_LEN)))
    live = dead_mask.astype(jnp.float32).reshape(1, channels)
    return pl.pallas_call(
        functools.partial(spectra_kernel, seg_count, window),
        out_shape=jax.ShapeDtypeStruct((seg_count, rows, channels), jnp.bfloat16),
        grid_spec=pltpu.PrefetchScalarGridSpec(
            num_scalar_prefetch=1,
            grid=(1,),
            in_specs=[
                pl.BlockSpec((rows, window), lambda i, offs: (0, 0)),
                pl.BlockSpec((1, channels), lambda i, offs: (0, 0)),
                pl.BlockSpec(memory_space=pl.ANY),
            ],
            out_specs=pl.BlockSpec((seg_count, rows, channels), lambda i, offs: (0, 0, 0)),
            scratch_shapes=[
                pltpu.VMEM((seg_count, window, channels), records.dtype),
                pltpu.SemaphoreType.DMA((seg_count,)),
            ],
        ),
        compiler_params=pltpu.CompilerParams(vmem_limit_bytes=56 * 1024 * 1024),
        cost_estimate=pl.CostEstimate(
            flops=2 * seg_count * rows * window * channels,
            bytes_accessed=seg_count * (window + rows) * channels * 2,
            transcendentals=seg_count * channels,
        ),
    )(offsets, padded, live, records)


def local_products(left_panel, partner_panels):
    seg_count = left_panel.shape[2]
    results = []
    for right_panel in partner_panels:
        turned = jnp.stack([-right_panel[:, 1], right_panel[:, 0]], axis=1)
        both = jnp.concatenate([right_panel, turned], axis=3)
        product = jnp.einsum(
            "fpsi,fpsj->fij", left_panel, both, preferred_element_type=jnp.float32
        )
        results.append(product * (1.0 / seg_count))
    return results


def neighbour_panels(own_panel):
    n_chan = lax.axis_size("chan")
    second_panel = from_behind(own_panel, "chan", -2)
    from_sibling = lax.ppermute(own_panel, "chan", [(c + 1, c) for c in range(0, n_chan, 2)])
    from_forward = lax.ppermute(second_panel, "chan", [(c - 1, c) for c in range(1, n_chan, 2)])
    odd = lax.axis_index("chan") % 2 == 1
    upper_panel = jnp.where(odd, from_forward, from_sibling)
    return upper_panel, second_panel, from_sibling


def shards(records, offsets, dead_mask, band_blocks):
    per_segment = whitened_spectra(records, offsets, dead_mask)
    seg_count, rows, channels = per_segment.shape
    whitened = per_segment.reshape(seg_count, BINS, 2, channels).transpose(1, 2, 0, 3)
    n_freq = lax.axis_size("freq")
    per_device = BINS // n_freq
    chunks = 2
    grouped = whitened.reshape(n_freq, chunks, per_device // chunks, 2, seg_count, channels)
    parts = [grouped[:, k].reshape(BINS // chunks, 2, seg_count, channels) for k in range(chunks)]
    chunk_products = []
    for k in range(chunks):
        own_panel = lax.all_to_all(parts[k], "freq", split_axis=0, concat_axis=2, tiled=True)
        upper_panel, second_panel, from_sibling = neighbour_panels(own_panel)
        if k + 1 < chunks:
            _, parts[k + 1] = lax.optimization_barrier((from_sibling, parts[k + 1]))
        chunk_products.append(local_products(own_panel, [own_panel, upper_panel, second_panel]))
    band_limit = band_blocks[0]
    results = []
    for offset_index in range(BAND + 1):
        product = jnp.concatenate([p[offset_index] for p in chunk_products], axis=0)
        keep_flag = (offset_index <= band_limit).astype(jnp.bfloat16)
        results.append(product.astype(jnp.bfloat16) * keep_flag)
    return jnp.stack(results, axis=0)


def solution(mesh):
    in_specs = (P("freq", "chan"), P("freq"), P("chan"), P("chan"))
    out_specs = P(None, "freq", "chan", None)
    return jax.shard_map(shards, mesh=mesh, in_specs=in_specs, out_specs=out_specs, check_vma=False)
```

```python
import functools

import jax
import jax.numpy as jnp
from jax import lax
from jax.experimental import pallas as pl
from jax.experimental.pallas import tpu as pltpu
from jax.sharding import PartitionSpec as P

SEG_LEN = 256
BINS = 32
FIRST_BIN = 2
BAND = 2


EPS_POWER = 1e-06


def from_behind(block, axis, distance):
    devices = range(lax.axis_size(axis))
    route = [(i - distance, i) for i in devices if i - distance in devices]
    return lax.ppermute(block, axis, route)


def dft_table(seg_length, bin_count, first_bin):
    sample_index = jnp.arange(seg_length, dtype=jnp.int32)
    row_index = jnp.arange(2 * bin_count, dtype=jnp.int32)
    harmonic = row_index // 2 + first_bin
    phase_steps = harmonic[:, None] * sample_index[None, :] % seg_length
    phase_angle = 2.0 * jnp.pi / seg_length * phase_steps.astype(jnp.float32)
    hann_taper = 0.5 - 0.5 * jnp.cos(2.0 * jnp.pi / seg_length * sample_index.astype(jnp.float32))
    wave_rows = jnp.where(
        (row_index % 2 == 0)[:, None], jnp.cos(phase_angle), -jnp.sin(phase_angle)
    )
    return (hann_taper[None, :] * wave_rows).astype(jnp.bfloat16)


def spectra_kernel(seg_count, window, offs_ref, dft_ref, mask_ref, rec_hbm, out_ref, frames, sems):
    last_start = rec_hbm.shape[0] - window
    starts = []
    copies = []
    for j in range(seg_count):
        offset = offs_ref[j]
        start = pl.multiple_of(jnp.minimum((offset // 16) * 16, last_start), 16)
        starts.append(offset - start)
        copies.append(
            pltpu.make_async_copy(rec_hbm.at[pl.ds(start, window)], frames.at[j], sems.at[j])
        )
    for copy in copies:
        copy.start()
    dft = dft_ref[...]
    live = mask_ref[...]
    for j in range(seg_count):
        shifted = pltpu.roll(dft, starts[j], 1).astype(jnp.bfloat16)
        copies[j].wait()
        spec = jnp.dot(shifted, frames[j], preferred_element_type=jnp.float32)
        power = jnp.sum(spec * spec, axis=0, keepdims=True) * (1.0 / BINS)
        scale = live / jnp.sqrt(power + EPS_POWER)
        out_ref[j] = (spec * scale).astype(out_ref.dtype)


def whitened_spectra(records, offsets, dead_mask):
    seg_count = offsets.shape[0]
    channels = records.shape[1]
    window = SEG_LEN + 128
    dft_rows = dft_table(SEG_LEN, BINS, FIRST_BIN)
    rows = dft_rows.shape[0]
    padded = jnp.pad(dft_rows.astype(jnp.float32), ((0, 0), (0, window - SEG_LEN)))
    live = dead_mask.astype(jnp.float32).reshape(1, channels)
    return pl.pallas_call(
        functools.partial(spectra_kernel, seg_count, window),
        out_shape=jax.ShapeDtypeStruct((seg_count, rows, channels), jnp.bfloat16),
        grid_spec=pltpu.PrefetchScalarGridSpec(
            num_scalar_prefetch=1,
            grid=(1,),
            in_specs=[
                pl.BlockSpec((rows, window), lambda i, offs: (0, 0)),
                pl.BlockSpec((1, channels), lambda i, offs: (0, 0)),
                pl.BlockSpec(memory_space=pl.ANY),
            ],
            out_specs=pl.BlockSpec((seg_count, rows, channels), lambda i, offs: (0, 0, 0)),
            scratch_shapes=[
                pltpu.VMEM((seg_count, window, channels), records.dtype),
                pltpu.SemaphoreType.DMA((seg_count,)),
            ],
        ),
        compiler_params=pltpu.CompilerParams(vmem_limit_bytes=56 * 1024 * 1024),
        cost_estimate=pl.CostEstimate(
            flops=2 * seg_count * rows * window * channels,
            bytes_accessed=seg_count * (window + rows) * channels * 2,
            transcendentals=seg_count * channels,
        ),
    )(offsets, padded, live, records)


def local_products(left_panel, partner_panels):
    seg_count = left_panel.shape[2]
    results = []
    for right_panel in partner_panels:
        turned = jnp.stack([-right_panel[:, 1], right_panel[:, 0]], axis=1)
        both = jnp.concatenate([right_panel, turned], axis=3)
        product = jnp.einsum(
            "fpsi,fpsj->fij", left_panel, both, preferred_element_type=jnp.float32
        )
        results.append(product * (1.0 / seg_count))
    return results


def neighbour_panels(own_panel):
    n_chan = lax.axis_size("chan")
    second_panel = from_behind(own_panel, "chan", -2)
    from_sibling = lax.ppermute(own_panel, "chan", [(c + 1, c) for c in range(0, n_chan, 2)])
    from_forward = lax.ppermute(second_panel, "chan", [(c - 1, c) for c in range(1, n_chan, 2)])
    odd = lax.axis_index("chan") % 2 == 1
    upper_panel = jnp.where(odd, from_forward, from_sibling)
    return upper_panel, second_panel, from_sibling


def shards(records, offsets, dead_mask, band_blocks):
    per_segment = whitened_spectra(records, offsets, dead_mask)
    seg_count, rows, channels = per_segment.shape
    whitened = per_segment.reshape(seg_count, BINS, 2, channels).transpose(1, 2, 0, 3)
    n_freq = lax.axis_size("freq")
    per_device = BINS // n_freq
    chunks = 1
    grouped = whitened.reshape(n_freq, chunks, per_device // chunks, 2, seg_count, channels)
    parts = [grouped[:, k].reshape(BINS // chunks, 2, seg_count, channels) for k in range(chunks)]
    chunk_products = []
    for k in range(chunks):
        own_panel = lax.all_to_all(parts[k], "freq", split_axis=0, concat_axis=2, tiled=True)
        upper_panel, second_panel, from_sibling = neighbour_panels(own_panel)
        if k + 1 < chunks:
            _, parts[k + 1] = lax.optimization_barrier((from_sibling, parts[k + 1]))
        chunk_products.append(local_products(own_panel, [own_panel, upper_panel, second_panel]))
    band_limit = band_blocks[0]
    results = []
    for offset_index in range(BAND + 1):
        product = jnp.concatenate([p[offset_index] for p in chunk_products], axis=0)
        keep_flag = (offset_index <= band_limit).astype(jnp.bfloat16)
        results.append(product.astype(jnp.bfloat16) * keep_flag)
    return jnp.stack(results, axis=0)


def solution(mesh):
    in_specs = (P("freq", "chan"), P("freq"), P("chan"), P("chan"))
    out_specs = P(None, "freq", "chan", None)
    return jax.shard_map(shards, mesh=mesh, in_specs=in_specs, out_specs=out_specs, check_vma=False)
```

```python
import functools

import jax
import jax.numpy as jnp
from jax import lax
from jax.experimental import pallas as pl
from jax.experimental.pallas import tpu as pltpu
from jax.sharding import PartitionSpec as P

SEG_LEN = 256
BINS = 32
FIRST_BIN = 2
BAND = 2


EPS_POWER = 1e-06


def from_behind(block, axis, distance):
    devices = range(lax.axis_size(axis))
    route = [(i - distance, i) for i in devices if i - distance in devices]
    return lax.ppermute(block, axis, route)


def dft_table(seg_length, bin_count, first_bin):
    sample_index = jnp.arange(seg_length, dtype=jnp.int32)
    row_index = jnp.arange(2 * bin_count, dtype=jnp.int32)
    harmonic = row_index // 2 + first_bin
    phase_steps = harmonic[:, None] * sample_index[None, :] % seg_length
    phase_angle = 2.0 * jnp.pi / seg_length * phase_steps.astype(jnp.float32)
    hann_taper = 0.5 - 0.5 * jnp.cos(2.0 * jnp.pi / seg_length * sample_index.astype(jnp.float32))
    wave_rows = jnp.where(
        (row_index % 2 == 0)[:, None], jnp.cos(phase_angle), -jnp.sin(phase_angle)
    )
    return (hann_taper[None, :] * wave_rows).astype(jnp.bfloat16)


def spectra_kernel(seg_count, window, offs_ref, dft_ref, mask_ref, rec_hbm, out_ref, frames, sems):
    last_start = rec_hbm.shape[0] - window
    starts = []
    copies = []
    for j in range(seg_count):
        offset = offs_ref[j]
        start = pl.multiple_of(jnp.minimum((offset // 16) * 16, last_start), 16)
        starts.append(offset - start)
        copies.append(
            pltpu.make_async_copy(rec_hbm.at[pl.ds(start, window)], frames.at[j], sems.at[j])
        )
    for copy in copies:
        copy.start()
    dft = dft_ref[...]
    live = mask_ref[...]
    for j in range(seg_count):
        shifted = pltpu.roll(dft, starts[j], 1).astype(jnp.bfloat16)
        copies[j].wait()
        spec = jnp.dot(shifted, frames[j], preferred_element_type=jnp.float32)
        power = jnp.sum(spec * spec, axis=0, keepdims=True) * (1.0 / BINS)
        scale = live / jnp.sqrt(power + EPS_POWER)
        out_ref[j] = (spec * scale).astype(out_ref.dtype)


def whitened_spectra(records, offsets, dead_mask):
    seg_count = offsets.shape[0]
    channels = records.shape[1]
    window = SEG_LEN + 128
    dft_rows = dft_table(SEG_LEN, BINS, FIRST_BIN)
    rows = dft_rows.shape[0]
    padded = jnp.pad(dft_rows.astype(jnp.float32), ((0, 0), (0, window - SEG_LEN)))
    live = dead_mask.astype(jnp.float32).reshape(1, channels)
    return pl.pallas_call(
        functools.partial(spectra_kernel, seg_count, window),
        out_shape=jax.ShapeDtypeStruct((seg_count, rows, channels), jnp.bfloat16),
        grid_spec=pltpu.PrefetchScalarGridSpec(
            num_scalar_prefetch=1,
            grid=(1,),
            in_specs=[
                pl.BlockSpec((rows, window), lambda i, offs: (0, 0)),
                pl.BlockSpec((1, channels), lambda i, offs: (0, 0)),
                pl.BlockSpec(memory_space=pl.ANY),
            ],
            out_specs=pl.BlockSpec((seg_count, rows, channels), lambda i, offs: (0, 0, 0)),
            scratch_shapes=[
                pltpu.VMEM((seg_count, window, channels), records.dtype),
                pltpu.SemaphoreType.DMA((seg_count,)),
            ],
        ),
        compiler_params=pltpu.CompilerParams(vmem_limit_bytes=56 * 1024 * 1024),
        cost_estimate=pl.CostEstimate(
            flops=2 * seg_count * rows * window * channels,
            bytes_accessed=seg_count * (window + rows) * channels * 2,
            transcendentals=seg_count * channels,
        ),
    )(offsets, padded, live, records)


def local_products(left_panel, partner_panels):
    seg_count = left_panel.shape[2]
    results = []
    for right_panel in partner_panels:
        turned = jnp.stack([-right_panel[:, 1], right_panel[:, 0]], axis=1)
        both = jnp.concatenate([right_panel, turned], axis=3)
        product = jnp.einsum(
            "fpsi,fpsj->fij", left_panel, both, preferred_element_type=jnp.float32
        )
        results.append(product * (1.0 / seg_count))
    return results


def neighbour_panels(own_panel):
    n_chan = lax.axis_size("chan")
    second_panel = from_behind(own_panel, "chan", -2)
    from_sibling = lax.ppermute(own_panel, "chan", [(c + 1, c) for c in range(0, n_chan, 2)])
    from_forward = lax.ppermute(second_panel, "chan", [(c - 1, c) for c in range(1, n_chan, 2)])
    odd = lax.axis_index("chan") % 2 == 1
    upper_panel = jnp.where(odd, from_forward, from_sibling)
    return upper_panel, second_panel, from_sibling


def shards(records, offsets, dead_mask, band_blocks):
    per_segment = whitened_spectra(records, offsets, dead_mask)
    seg_count, rows, channels = per_segment.shape
    whitened = per_segment.reshape(seg_count, BINS, 2, channels).transpose(1, 2, 0, 3)
    n_freq = lax.axis_size("freq")
    per_device = BINS // n_freq
    sizes = [1, per_device - 1]
    chunks = len(sizes)
    grouped = whitened.reshape(n_freq, per_device, 2, seg_count, channels)
    bounds = [sum(sizes[:k]) for k in range(chunks + 1)]
    parts = [
        grouped[:, bounds[k]:bounds[k + 1]].reshape(n_freq * sizes[k], 2, seg_count, channels)
        for k in range(chunks)
    ]
    chunk_products = []
    for k in range(chunks):
        own_panel = lax.all_to_all(parts[k], "freq", split_axis=0, concat_axis=2, tiled=True)
        upper_panel, second_panel, from_sibling = neighbour_panels(own_panel)
        if k + 1 < chunks:
            _, parts[k + 1] = lax.optimization_barrier((from_sibling, parts[k + 1]))
        chunk_products.append(local_products(own_panel, [own_panel, upper_panel, second_panel]))
    band_limit = band_blocks[0]
    results = []
    for offset_index in range(BAND + 1):
        product = jnp.concatenate([p[offset_index] for p in chunk_products], axis=0)
        keep_flag = (offset_index <= band_limit).astype(jnp.bfloat16)
        results.append(product.astype(jnp.bfloat16) * keep_flag)
    return jnp.stack(results, axis=0)


def solution(mesh):
    in_specs = (P("freq", "chan"), P("freq"), P("chan"), P("chan"))
    out_specs = P(None, "freq", "chan", None)
    return jax.shard_map(shards, mesh=mesh, in_specs=in_specs, out_specs=out_specs, check_vma=False)
```

```python
import functools

import jax
import jax.numpy as jnp
from jax import lax
from jax.experimental import pallas as pl
from jax.experimental.pallas import tpu as pltpu
from jax.sharding import PartitionSpec as P

SEG_LEN = 256
BINS = 32
FIRST_BIN = 2
BAND = 2


EPS_POWER = 1e-06


def from_behind(block, axis, distance):
    devices = range(lax.axis_size(axis))
    route = [(i - distance, i) for i in devices if i - distance in devices]
    return lax.ppermute(block, axis, route)


def dft_table(seg_length, bin_count, first_bin):
    sample_index = jnp.arange(seg_length, dtype=jnp.int32)
    row_index = jnp.arange(2 * bin_count, dtype=jnp.int32)
    harmonic = row_index // 2 + first_bin
    phase_steps = harmonic[:, None] * sample_index[None, :] % seg_length
    phase_angle = 2.0 * jnp.pi / seg_length * phase_steps.astype(jnp.float32)
    hann_taper = 0.5 - 0.5 * jnp.cos(2.0 * jnp.pi / seg_length * sample_index.astype(jnp.float32))
    wave_rows = jnp.where(
        (row_index % 2 == 0)[:, None], jnp.cos(phase_angle), -jnp.sin(phase_angle)
    )
    return (hann_taper[None, :] * wave_rows).astype(jnp.bfloat16)


def spectra_kernel(seg_count, window, offs_ref, dft_ref, mask_ref, rec_hbm, out_ref, frames, sems):
    last_start = rec_hbm.shape[0] - window
    starts = []
    copies = []
    for j in range(seg_count):
        offset = offs_ref[j]
        start = pl.multiple_of(jnp.minimum((offset // 16) * 16, last_start), 16)
        starts.append(offset - start)
        copies.append(
            pltpu.make_async_copy(rec_hbm.at[pl.ds(start, window)], frames.at[j], sems.at[j])
        )
    for copy in copies:
        copy.start()
    dft = dft_ref[...]
    live = mask_ref[...]
    for j in range(seg_count):
        shifted = pltpu.roll(dft, starts[j], 1).astype(jnp.bfloat16)
        copies[j].wait()
        spec = jnp.dot(shifted, frames[j], preferred_element_type=jnp.float32)
        power = jnp.sum(spec * spec, axis=0, keepdims=True) * (1.0 / BINS)
        scale = live / jnp.sqrt(power + EPS_POWER)
        out_ref[j] = (spec * scale).astype(out_ref.dtype)


def whitened_spectra(records, offsets, dead_mask, dft_rows):
    seg_count = offsets.shape[0]
    channels = records.shape[1]
    window = SEG_LEN + 128
    rows = dft_rows.shape[0]
    padded = jnp.pad(dft_rows.astype(jnp.float32), ((0, 0), (0, window - SEG_LEN)))
    live = dead_mask.astype(jnp.float32).reshape(1, channels)
    return pl.pallas_call(
        functools.partial(spectra_kernel, seg_count, window),
        out_shape=jax.ShapeDtypeStruct((seg_count, rows, channels), jnp.bfloat16),
        grid_spec=pltpu.PrefetchScalarGridSpec(
            num_scalar_prefetch=1,
            grid=(1,),
            in_specs=[
                pl.BlockSpec((rows, window), lambda i, offs: (0, 0)),
                pl.BlockSpec((1, channels), lambda i, offs: (0, 0)),
                pl.BlockSpec(memory_space=pl.ANY),
            ],
            out_specs=pl.BlockSpec((seg_count, rows, channels), lambda i, offs: (0, 0, 0)),
            scratch_shapes=[
                pltpu.VMEM((seg_count, window, channels), records.dtype),
                pltpu.SemaphoreType.DMA((seg_count,)),
            ],
        ),
        compiler_params=pltpu.CompilerParams(vmem_limit_bytes=56 * 1024 * 1024),
        cost_estimate=pl.CostEstimate(
            flops=2 * seg_count * rows * window * channels,
            bytes_accessed=seg_count * (window + rows) * channels * 2,
            transcendentals=seg_count * channels,
        ),
    )(offsets, padded, live, records)


def local_products(left_panel, partner_panels):
    seg_count = left_panel.shape[2]
    results = []
    for right_panel in partner_panels:
        turned = jnp.stack([-right_panel[:, 1], right_panel[:, 0]], axis=1)
        both = jnp.concatenate([right_panel, turned], axis=3)
        product = jnp.einsum(
            "fpsi,fpsj->fij", left_panel, both, preferred_element_type=jnp.float32
        )
        results.append(product * (1.0 / seg_count))
    return results


def neighbour_panels(own_panel):
    n_chan = lax.axis_size("chan")
    second_panel = from_behind(own_panel, "chan", -2)
    from_sibling = lax.ppermute(own_panel, "chan", [(c + 1, c) for c in range(0, n_chan, 2)])
    from_forward = lax.ppermute(second_panel, "chan", [(c - 1, c) for c in range(1, n_chan, 2)])
    odd = lax.axis_index("chan") % 2 == 1
    upper_panel = jnp.where(odd, from_forward, from_sibling)
    return upper_panel, second_panel, from_sibling


def shards(records, offsets, dead_mask, band_blocks):
    n_freq = lax.axis_size("freq")
    per_device = BINS // n_freq
    chunks = 2
    per_chunk = per_device // chunks
    table = dft_table(SEG_LEN, BINS, FIRST_BIN).reshape(n_freq, chunks, per_chunk, 2, SEG_LEN)
    table = table.transpose(3, 1, 0, 2, 4).reshape(2 * BINS, SEG_LEN)
    per_segment = whitened_spectra(records, offsets, dead_mask, table)
    seg_count, rows, channels = per_segment.shape
    slabs = per_segment.reshape(seg_count, 2, chunks, n_freq * per_chunk, channels)
    parts = [slabs[:, :, k].transpose(2, 1, 0, 3) for k in range(chunks)]
    chunk_products = []
    for k in range(chunks):
        own_panel = lax.all_to_all(parts[k], "freq", split_axis=0, concat_axis=2, tiled=True)
        upper_panel, second_panel, from_sibling = neighbour_panels(own_panel)
        if k + 1 < chunks:
            _, parts[k + 1] = lax.optimization_barrier((from_sibling, parts[k + 1]))
        chunk_products.append(local_products(own_panel, [own_panel, upper_panel, second_panel]))
    band_limit = band_blocks[0]
    results = []
    for offset_index in range(BAND + 1):
        product = jnp.concatenate([p[offset_index] for p in chunk_products], axis=0)
        keep_flag = (offset_index <= band_limit).astype(jnp.bfloat16)
        results.append(product.astype(jnp.bfloat16) * keep_flag)
    return jnp.stack(results, axis=0)


def solution(mesh):
    in_specs = (P("freq", "chan"), P("freq"), P("chan"), P("chan"))
    out_specs = P(None, "freq", "chan", None)
    return jax.shard_map(shards, mesh=mesh, in_specs=in_specs, out_specs=out_specs, check_vma=False)
```

```python
import functools

import jax
import jax.numpy as jnp
from jax import lax
from jax.experimental import pallas as pl
from jax.experimental.pallas import tpu as pltpu
from jax.sharding import PartitionSpec as P

SEG_LEN = 256
BINS = 32
FIRST_BIN = 2
BAND = 2


EPS_POWER = 1e-06


def from_behind(block, axis, distance):
    devices = range(lax.axis_size(axis))
    route = [(i - distance, i) for i in devices if i - distance in devices]
    return lax.ppermute(block, axis, route)


def dft_table(seg_length, bin_count, first_bin):
    sample_index = jnp.arange(seg_length, dtype=jnp.int32)
    row_index = jnp.arange(2 * bin_count, dtype=jnp.int32)
    harmonic = row_index // 2 + first_bin
    phase_steps = harmonic[:, None] * sample_index[None, :] % seg_length
    phase_angle = 2.0 * jnp.pi / seg_length * phase_steps.astype(jnp.float32)
    hann_taper = 0.5 - 0.5 * jnp.cos(2.0 * jnp.pi / seg_length * sample_index.astype(jnp.float32))
    wave_rows = jnp.where(
        (row_index % 2 == 0)[:, None], jnp.cos(phase_angle), -jnp.sin(phase_angle)
    )
    return (hann_taper[None, :] * wave_rows).astype(jnp.bfloat16)


def spectra_kernel(seg_count, window, offs_ref, dft_ref, mask_ref, rec_hbm, out_ref, frames, sems):
    last_start = rec_hbm.shape[0] - window
    starts = []
    copies = []
    for j in range(seg_count):
        offset = offs_ref[j]
        start = pl.multiple_of(jnp.minimum((offset // 16) * 16, last_start), 16)
        starts.append(offset - start)
        copies.append(
            pltpu.make_async_copy(rec_hbm.at[pl.ds(start, window)], frames.at[j], sems.at[j])
        )
    for copy in copies:
        copy.start()
    dft = dft_ref[...]
    live = mask_ref[...]
    for j in range(seg_count):
        shifted = pltpu.roll(dft, starts[j], 1).astype(jnp.bfloat16)
        copies[j].wait()
        spec = jnp.dot(shifted, frames[j], preferred_element_type=jnp.float32)
        power = jnp.sum(spec * spec, axis=0, keepdims=True) * (1.0 / BINS)
        scale = live / jnp.sqrt(power + EPS_POWER)
        out_ref[j] = (spec * scale).astype(out_ref.dtype)


def whitened_spectra(records, offsets, dead_mask, dft_rows):
    seg_count = offsets.shape[0]
    channels = records.shape[1]
    window = SEG_LEN + 128
    rows = dft_rows.shape[0]
    padded = jnp.pad(dft_rows.astype(jnp.float32), ((0, 0), (0, window - SEG_LEN)))
    live = dead_mask.astype(jnp.float32).reshape(1, channels)
    return pl.pallas_call(
        functools.partial(spectra_kernel, seg_count, window),
        out_shape=jax.ShapeDtypeStruct((seg_count, rows, channels), jnp.bfloat16),
        grid_spec=pltpu.PrefetchScalarGridSpec(
            num_scalar_prefetch=1,
            grid=(1,),
            in_specs=[
                pl.BlockSpec((rows, window), lambda i, offs: (0, 0)),
                pl.BlockSpec((1, channels), lambda i, offs: (0, 0)),
                pl.BlockSpec(memory_space=pl.ANY),
            ],
            out_specs=pl.BlockSpec((seg_count, rows, channels), lambda i, offs: (0, 0, 0)),
            scratch_shapes=[
                pltpu.VMEM((seg_count, window, channels), records.dtype),
                pltpu.SemaphoreType.DMA((seg_count,)),
            ],
        ),
        compiler_params=pltpu.CompilerParams(vmem_limit_bytes=56 * 1024 * 1024),
        cost_estimate=pl.CostEstimate(
            flops=2 * seg_count * rows * window * channels,
            bytes_accessed=seg_count * (window + rows) * channels * 2,
            transcendentals=seg_count * channels,
        ),
    )(offsets, padded, live, records)


def local_products(left_panel, partner_panels):
    seg_count = left_panel.shape[2]
    results = []
    for right_panel in partner_panels:
        turned = jnp.stack([-right_panel[:, 1], right_panel[:, 0]], axis=1)
        both = jnp.concatenate([right_panel, turned], axis=3)
        product = jnp.einsum(
            "fpsi,fpsj->fij", left_panel, both, preferred_element_type=jnp.float32
        )
        results.append(product * (1.0 / seg_count))
    return results


def neighbour_panels(own_panel):
    n_chan = lax.axis_size("chan")
    second_panel = from_behind(own_panel, "chan", -2)
    from_sibling = lax.ppermute(own_panel, "chan", [(c + 1, c) for c in range(0, n_chan, 2)])
    from_forward = lax.ppermute(second_panel, "chan", [(c - 1, c) for c in range(1, n_chan, 2)])
    odd = lax.axis_index("chan") % 2 == 1
    upper_panel = jnp.where(odd, from_forward, from_sibling)
    return upper_panel, second_panel, from_sibling


def shards(records, offsets, dead_mask, band_blocks):
    n_freq = lax.axis_size("freq")
    per_device = BINS // n_freq
    sizes = [per_device - 1, 1]
    chunks = len(sizes)
    bounds = [sum(sizes[:k]) for k in range(chunks + 1)]
    table = dft_table(SEG_LEN, BINS, FIRST_BIN).reshape(n_freq, per_device, 2, SEG_LEN)
    table = jnp.concatenate(
        [table[:, bounds[k]:bounds[k + 1]].reshape(n_freq * sizes[k], 2, SEG_LEN) for k in range(chunks)], axis=0
    )
    table = table.transpose(1, 0, 2).reshape(2 * BINS, SEG_LEN)
    per_segment = whitened_spectra(records, offsets, dead_mask, table)
    seg_count, rows, channels = per_segment.shape
    slabs = per_segment.reshape(seg_count, 2, BINS, channels)
    parts = [
        slabs[:, :, n_freq * bounds[k]:n_freq * bounds[k + 1]].transpose(2, 1, 0, 3) for k in range(chunks)
    ]
    chunk_products = []
    for k in range(chunks):
        own_panel = lax.all_to_all(parts[k], "freq", split_axis=0, concat_axis=2, tiled=True)
        upper_panel, second_panel, from_sibling = neighbour_panels(own_panel)
        if k + 1 < chunks:
            _, parts[k + 1] = lax.optimization_barrier((from_sibling, parts[k + 1]))
        chunk_products.append(local_products(own_panel, [own_panel, upper_panel, second_panel]))
    band_limit = band_blocks[0]
    results = []
    for offset_index in range(BAND + 1):
        product = jnp.concatenate([p[offset_index] for p in chunk_products], axis=0)
        keep_flag = (offset_index <= band_limit).astype(jnp.bfloat16)
        results.append(product.astype(jnp.bfloat16) * keep_flag)
    return jnp.stack(results, axis=0)


def solution(mesh):
    in_specs = (P("freq", "chan"), P("freq"), P("chan"), P("chan"))
    out_specs = P(None, "freq", "chan", None)
    return jax.shard_map(shards, mesh=mesh, in_specs=in_specs, out_specs=out_specs, check_vma=False)
```

```python
import functools

import jax
import jax.numpy as jnp
from jax import lax
from jax.experimental import pallas as pl
from jax.experimental.pallas import tpu as pltpu
from jax.sharding import PartitionSpec as P

SEG_LEN = 256
BINS = 32
FIRST_BIN = 2
BAND = 2


EPS_POWER = 1e-06


def from_behind(block, axis, distance):
    devices = range(lax.axis_size(axis))
    route = [(i - distance, i) for i in devices if i - distance in devices]
    return lax.ppermute(block, axis, route)


def dft_table(seg_length, bin_count, first_bin):
    sample_index = jnp.arange(seg_length, dtype=jnp.int32)
    row_index = jnp.arange(2 * bin_count, dtype=jnp.int32)
    harmonic = row_index // 2 + first_bin
    phase_steps = harmonic[:, None] * sample_index[None, :] % seg_length
    phase_angle = 2.0 * jnp.pi / seg_length * phase_steps.astype(jnp.float32)
    hann_taper = 0.5 - 0.5 * jnp.cos(2.0 * jnp.pi / seg_length * sample_index.astype(jnp.float32))
    wave_rows = jnp.where(
        (row_index % 2 == 0)[:, None], jnp.cos(phase_angle), -jnp.sin(phase_angle)
    )
    return (hann_taper[None, :] * wave_rows).astype(jnp.bfloat16)


def spectra_kernel(seg_count, window, offs_ref, dft_ref, mask_ref, rec_hbm, out_ref, frames, sems):
    last_start = rec_hbm.shape[0] - window
    starts = []
    copies = []
    for j in range(seg_count):
        offset = offs_ref[j]
        start = pl.multiple_of(jnp.minimum((offset // 16) * 16, last_start), 16)
        starts.append(offset - start)
        copies.append(
            pltpu.make_async_copy(rec_hbm.at[pl.ds(start, window)], frames.at[j], sems.at[j])
        )
    for copy in copies:
        copy.start()
    dft = dft_ref[...]
    live = mask_ref[...]
    for j in range(seg_count):
        shifted = pltpu.roll(dft, starts[j], 1).astype(jnp.bfloat16)
        copies[j].wait()
        spec = jnp.dot(shifted, frames[j], preferred_element_type=jnp.float32)
        power = jnp.sum(spec * spec, axis=0, keepdims=True) * (1.0 / BINS)
        scale = live / jnp.sqrt(power + EPS_POWER)
        out_ref[j] = (spec * scale).astype(out_ref.dtype)


def whitened_spectra(records, offsets, dead_mask, dft_rows):
    seg_count = offsets.shape[0]
    channels = records.shape[1]
    window = SEG_LEN + 128
    rows = dft_rows.shape[0]
    padded = jnp.pad(dft_rows.astype(jnp.float32), ((0, 0), (0, window - SEG_LEN)))
    live = dead_mask.astype(jnp.float32).reshape(1, channels)
    return pl.pallas_call(
        functools.partial(spectra_kernel, seg_count, window),
        out_shape=jax.ShapeDtypeStruct((seg_count, rows, channels), jnp.bfloat16),
        grid_spec=pltpu.PrefetchScalarGridSpec(
            num_scalar_prefetch=1,
            grid=(1,),
            in_specs=[
                pl.BlockSpec((rows, window), lambda i, offs: (0, 0)),
                pl.BlockSpec((1, channels), lambda i, offs: (0, 0)),
                pl.BlockSpec(memory_space=pl.ANY),
            ],
            out_specs=pl.BlockSpec((seg_count, rows, channels), lambda i, offs: (0, 0, 0)),
            scratch_shapes=[
                pltpu.VMEM((seg_count, window, channels), records.dtype),
                pltpu.SemaphoreType.DMA((seg_count,)),
            ],
        ),
        compiler_params=pltpu.CompilerParams(vmem_limit_bytes=56 * 1024 * 1024),
        cost_estimate=pl.CostEstimate(
            flops=2 * seg_count * rows * window * channels,
            bytes_accessed=seg_count * (window + rows) * channels * 2,
            transcendentals=seg_count * channels,
        ),
    )(offsets, padded, live, records)


def local_products(left_panel, partner_panels):
    seg_count = left_panel.shape[2]
    results = []
    for right_panel in partner_panels:
        turned = jnp.stack([-right_panel[:, 1], right_panel[:, 0]], axis=1)
        both = jnp.concatenate([right_panel, turned], axis=3)
        product = jnp.einsum(
            "fpsi,fpsj->fij", left_panel, both, preferred_element_type=jnp.float32
        )
        results.append(product * (1.0 / seg_count))
    return results


def neighbour_panels(own_panel, flows=1):
    n_chan = lax.axis_size("chan")
    if flows == 1:
        second_panel = from_behind(own_panel, "chan", -2)
    else:
        second_panel = jnp.concatenate(
            [from_behind(own_panel[b:b + 1], "chan", -2) for b in range(own_panel.shape[0])], axis=0
        )
    from_sibling = lax.ppermute(own_panel, "chan", [(c + 1, c) for c in range(0, n_chan, 2)])
    from_forward = lax.ppermute(second_panel, "chan", [(c - 1, c) for c in range(1, n_chan, 2)])
    odd = lax.axis_index("chan") % 2 == 1
    upper_panel = jnp.where(odd, from_forward, from_sibling)
    return upper_panel, second_panel, from_sibling


def shards(records, offsets, dead_mask, band_blocks):
    n_freq = lax.axis_size("freq")
    per_device = BINS // n_freq
    chunks = 2
    per_chunk = per_device // chunks
    table = dft_table(SEG_LEN, BINS, FIRST_BIN).reshape(n_freq, chunks, per_chunk, 2, SEG_LEN)
    table = table.transpose(3, 1, 0, 2, 4).reshape(2 * BINS, SEG_LEN)
    per_segment = whitened_spectra(records, offsets, dead_mask, table)
    seg_count, rows, channels = per_segment.shape
    slabs = per_segment.reshape(seg_count, 2, chunks, n_freq * per_chunk, channels)
    parts = [slabs[:, :, k].transpose(2, 1, 0, 3) for k in range(chunks)]
    chunk_products = []
    for k in range(chunks):
        own_panel = lax.all_to_all(parts[k], "freq", split_axis=0, concat_axis=2, tiled=True)
        upper_panel, second_panel, from_sibling = neighbour_panels(own_panel, 1 if k + 1 < chunks else 2)
        if k + 1 < chunks:
            _, parts[k + 1] = lax.optimization_barrier((from_sibling, parts[k + 1]))
        chunk_products.append(local_products(own_panel, [own_panel, upper_panel, second_panel]))
    band_limit = band_blocks[0]
    results = []
    for offset_index in range(BAND + 1):
        product = jnp.concatenate([p[offset_index] for p in chunk_products], axis=0)
        keep_flag = (offset_index <= band_limit).astype(jnp.bfloat16)
        results.append(product.astype(jnp.bfloat16) * keep_flag)
    return jnp.stack(results, axis=0)


def solution(mesh):
    in_specs = (P("freq", "chan"), P("freq"), P("chan"), P("chan"))
    out_specs = P(None, "freq", "chan", None)
    return jax.shard_map(shards, mesh=mesh, in_specs=in_specs, out_specs=out_specs, check_vma=False)
```

```python
import functools

import jax
import jax.numpy as jnp
from jax import lax
from jax.experimental import pallas as pl
from jax.experimental.pallas import tpu as pltpu
from jax.sharding import PartitionSpec as P

SEG_LEN = 256
BINS = 32
FIRST_BIN = 2
BAND = 2


EPS_POWER = 1e-06


def from_behind(block, axis, distance):
    devices = range(lax.axis_size(axis))
    route = [(i - distance, i) for i in devices if i - distance in devices]
    return lax.ppermute(block, axis, route)


def dft_table(seg_length, bin_count, first_bin):
    sample_index = jnp.arange(seg_length, dtype=jnp.int32)
    row_index = jnp.arange(2 * bin_count, dtype=jnp.int32)
    harmonic = row_index // 2 + first_bin
    phase_steps = harmonic[:, None] * sample_index[None, :] % seg_length
    phase_angle = 2.0 * jnp.pi / seg_length * phase_steps.astype(jnp.float32)
    hann_taper = 0.5 - 0.5 * jnp.cos(2.0 * jnp.pi / seg_length * sample_index.astype(jnp.float32))
    wave_rows = jnp.where(
        (row_index % 2 == 0)[:, None], jnp.cos(phase_angle), -jnp.sin(phase_angle)
    )
    return (hann_taper[None, :] * wave_rows).astype(jnp.bfloat16)


def spectra_kernel(seg_count, window, offs_ref, dft_ref, mask_ref, rec_hbm, out_ref, frames, sems):
    last_start = rec_hbm.shape[0] - window
    starts = []
    copies = []
    for j in range(seg_count):
        offset = offs_ref[j]
        start = pl.multiple_of(jnp.minimum((offset // 16) * 16, last_start), 16)
        starts.append(offset - start)
        copies.append(
            pltpu.make_async_copy(rec_hbm.at[pl.ds(start, window)], frames.at[j], sems.at[j])
        )
    for copy in copies:
        copy.start()
    dft = dft_ref[...]
    live = mask_ref[...]
    for j in range(seg_count):
        shifted = pltpu.roll(dft, starts[j], 1).astype(jnp.bfloat16)
        copies[j].wait()
        spec = jnp.dot(shifted, frames[j], preferred_element_type=jnp.float32)
        power = jnp.sum(spec * spec, axis=0, keepdims=True) * (1.0 / BINS)
        scale = live / jnp.sqrt(power + EPS_POWER)
        out_ref[j] = (spec * scale).astype(out_ref.dtype)


def whitened_spectra(records, offsets, dead_mask, dft_rows):
    seg_count = offsets.shape[0]
    channels = records.shape[1]
    window = SEG_LEN + 128
    rows = dft_rows.shape[0]
    padded = jnp.pad(dft_rows.astype(jnp.float32), ((0, 0), (0, window - SEG_LEN)))
    live = dead_mask.astype(jnp.float32).reshape(1, channels)
    return pl.pallas_call(
        functools.partial(spectra_kernel, seg_count, window),
        out_shape=jax.ShapeDtypeStruct((seg_count, rows, channels), jnp.bfloat16),
        grid_spec=pltpu.PrefetchScalarGridSpec(
            num_scalar_prefetch=1,
            grid=(1,),
            in_specs=[
                pl.BlockSpec((rows, window), lambda i, offs: (0, 0)),
                pl.BlockSpec((1, channels), lambda i, offs: (0, 0)),
                pl.BlockSpec(memory_space=pl.ANY),
            ],
            out_specs=pl.BlockSpec((seg_count, rows, channels), lambda i, offs: (0, 0, 0)),
            scratch_shapes=[
                pltpu.VMEM((seg_count, window, channels), records.dtype),
                pltpu.SemaphoreType.DMA((seg_count,)),
            ],
        ),
        compiler_params=pltpu.CompilerParams(vmem_limit_bytes=56 * 1024 * 1024),
        cost_estimate=pl.CostEstimate(
            flops=2 * seg_count * rows * window * channels,
            bytes_accessed=seg_count * (window + rows) * channels * 2,
            transcendentals=seg_count * channels,
        ),
    )(offsets, padded, live, records)


def local_products(left_panel, partner_panels):
    seg_count = left_panel.shape[2]
    results = []
    for right_panel in partner_panels:
        turned = jnp.stack([-right_panel[:, 1], right_panel[:, 0]], axis=1)
        both = jnp.concatenate([right_panel, turned], axis=3)
        product = jnp.einsum(
            "fpsi,fpsj->fij", left_panel, both, preferred_element_type=jnp.float32
        )
        results.append(product * (1.0 / seg_count))
    return results


def neighbour_panels(own_panel):
    n_chan = lax.axis_size("chan")
    second_panel = from_behind(own_panel, "chan", -2)
    from_sibling = lax.ppermute(own_panel, "chan", [(c + 1, c) for c in range(0, n_chan, 2)])
    from_forward = lax.ppermute(second_panel, "chan", [(c - 1, c) for c in range(1, n_chan, 2)])
    odd = lax.axis_index("chan") % 2 == 1
    upper_panel = jnp.where(odd, from_forward, from_sibling)
    return upper_panel, second_panel, from_sibling


def shards(records, offsets, dead_mask, band_blocks):
    n_freq = lax.axis_size("freq")
    per_device = BINS // n_freq
    chunks = 4
    per_chunk = per_device // chunks
    table = dft_table(SEG_LEN, BINS, FIRST_BIN).reshape(n_freq, chunks, per_chunk, 2, SEG_LEN)
    table = table.transpose(3, 1, 0, 2, 4).reshape(2 * BINS, SEG_LEN)
    per_segment = whitened_spectra(records, offsets, dead_mask, table)
    seg_count, rows, channels = per_segment.shape
    slabs = per_segment.reshape(seg_count, 2, chunks, n_freq * per_chunk, channels)
    parts = [slabs[:, :, k].transpose(2, 1, 0, 3) for k in range(chunks)]
    chunk_products = []
    for k in range(chunks):
        own_panel = lax.all_to_all(parts[k], "freq", split_axis=0, concat_axis=2, tiled=True)
        upper_panel, second_panel, from_sibling = neighbour_panels(own_panel)
        if k + 1 < chunks:
            _, parts[k + 1] = lax.optimization_barrier((from_sibling, parts[k + 1]))
        chunk_products.append(local_products(own_panel, [own_panel, upper_panel, second_panel]))
    band_limit = band_blocks[0]
    results = []
    for offset_index in range(BAND + 1):
        product = jnp.concatenate([p[offset_index] for p in chunk_products], axis=0)
        keep_flag = (offset_index <= band_limit).astype(jnp.bfloat16)
        results.append(product.astype(jnp.bfloat16) * keep_flag)
    return jnp.stack(results, axis=0)


def solution(mesh):
    in_specs = (P("freq", "chan"), P("freq"), P("chan"), P("chan"))
    out_specs = P(None, "freq", "chan", None)
    return jax.shard_map(shards, mesh=mesh, in_specs=in_specs, out_specs=out_specs, check_vma=False)
```

```python
import functools

import jax
import jax.numpy as jnp
from jax import lax
from jax.experimental import pallas as pl
from jax.experimental.pallas import tpu as pltpu
from jax.sharding import PartitionSpec as P

SEG_LEN = 256
BINS = 32
FIRST_BIN = 2
BAND = 2


EPS_POWER = 1e-06


def from_behind(block, axis, distance):
    devices = range(lax.axis_size(axis))
    route = [(i - distance, i) for i in devices if i - distance in devices]
    return lax.ppermute(block, axis, route)


def dft_table(seg_length, bin_count, first_bin):
    sample_index = jnp.arange(seg_length, dtype=jnp.int32)
    row_index = jnp.arange(2 * bin_count, dtype=jnp.int32)
    harmonic = row_index // 2 + first_bin
    phase_steps = harmonic[:, None] * sample_index[None, :] % seg_length
    phase_angle = 2.0 * jnp.pi / seg_length * phase_steps.astype(jnp.float32)
    hann_taper = 0.5 - 0.5 * jnp.cos(2.0 * jnp.pi / seg_length * sample_index.astype(jnp.float32))
    wave_rows = jnp.where(
        (row_index % 2 == 0)[:, None], jnp.cos(phase_angle), -jnp.sin(phase_angle)
    )
    return (hann_taper[None, :] * wave_rows).astype(jnp.bfloat16)


def spectra_kernel(seg_count, window, offs_ref, dft_ref, mask_ref, rec_hbm, out_ref, frames, sems):
    last_start = rec_hbm.shape[0] - window
    starts = []
    copies = []
    for j in range(seg_count):
        offset = offs_ref[j]
        start = pl.multiple_of(jnp.minimum((offset // 16) * 16, last_start), 16)
        starts.append(offset - start)
        copies.append(
            pltpu.make_async_copy(rec_hbm.at[pl.ds(start, window)], frames.at[j], sems.at[j])
        )
    for copy in copies:
        copy.start()
    dft = dft_ref[...]
    live = mask_ref[...]
    for j in range(seg_count):
        shifted = pltpu.roll(dft, starts[j], 1)[:, :window].astype(jnp.bfloat16)
        copies[j].wait()
        spec = jnp.dot(shifted, frames[j], preferred_element_type=jnp.float32)
        power = jnp.sum(spec * spec, axis=0, keepdims=True) * (1.0 / BINS)
        scale = live / jnp.sqrt(power + EPS_POWER)
        out_ref[j] = (spec * scale).astype(out_ref.dtype)


def whitened_spectra(records, offsets, dead_mask, dft_rows):
    seg_count = offsets.shape[0]
    channels = records.shape[1]
    window = SEG_LEN + 16
    rows = dft_rows.shape[0]
    padded = jnp.pad(dft_rows.astype(jnp.float32), ((0, 0), (0, 128)))
    live = dead_mask.astype(jnp.float32).reshape(1, channels)
    return pl.pallas_call(
        functools.partial(spectra_kernel, seg_count, window),
        out_shape=jax.ShapeDtypeStruct((seg_count, rows, channels), jnp.bfloat16),
        grid_spec=pltpu.PrefetchScalarGridSpec(
            num_scalar_prefetch=1,
            grid=(1,),
            in_specs=[
                pl.BlockSpec((rows, SEG_LEN + 128), lambda i, offs: (0, 0)),
                pl.BlockSpec((1, channels), lambda i, offs: (0, 0)),
                pl.BlockSpec(memory_space=pl.ANY),
            ],
            out_specs=pl.BlockSpec((seg_count, rows, channels), lambda i, offs: (0, 0, 0)),
            scratch_shapes=[
                pltpu.VMEM((seg_count, window, channels), records.dtype),
                pltpu.SemaphoreType.DMA((seg_count,)),
            ],
        ),
        compiler_params=pltpu.CompilerParams(vmem_limit_bytes=56 * 1024 * 1024),
        cost_estimate=pl.CostEstimate(
            flops=2 * seg_count * rows * window * channels,
            bytes_accessed=seg_count * (window + rows) * channels * 2,
            transcendentals=seg_count * channels,
        ),
    )(offsets, padded, live, records)


def local_products(left_panel, partner_panels):
    seg_count = left_panel.shape[2]
    results = []
    for right_panel in partner_panels:
        turned = jnp.stack([-right_panel[:, 1], right_panel[:, 0]], axis=1)
        both = jnp.concatenate([right_panel, turned], axis=3)
        product = jnp.einsum(
            "fpsi,fpsj->fij", left_panel, both, preferred_element_type=jnp.float32
        )
        results.append(product * (1.0 / seg_count))
    return results


def neighbour_panels(own_panel):
    n_chan = lax.axis_size("chan")
    second_panel = from_behind(own_panel, "chan", -2)
    from_sibling = lax.ppermute(own_panel, "chan", [(c + 1, c) for c in range(0, n_chan, 2)])
    from_forward = lax.ppermute(second_panel, "chan", [(c - 1, c) for c in range(1, n_chan, 2)])
    odd = lax.axis_index("chan") % 2 == 1
    upper_panel = jnp.where(odd, from_forward, from_sibling)
    return upper_panel, second_panel, from_sibling


def shards(records, offsets, dead_mask, band_blocks):
    n_freq = lax.axis_size("freq")
    per_device = BINS // n_freq
    chunks = 2
    per_chunk = per_device // chunks
    table = dft_table(SEG_LEN, BINS, FIRST_BIN).reshape(n_freq, chunks, per_chunk, 2, SEG_LEN)
    table = table.transpose(3, 1, 0, 2, 4).reshape(2 * BINS, SEG_LEN)
    per_segment = whitened_spectra(records, offsets, dead_mask, table)
    seg_count, rows, channels = per_segment.shape
    slabs = per_segment.reshape(seg_count, 2, chunks, n_freq * per_chunk, channels)
    parts = [slabs[:, :, k].transpose(2, 1, 0, 3) for k in range(chunks)]
    chunk_products = []
    for k in range(chunks):
        own_panel = lax.all_to_all(parts[k], "freq", split_axis=0, concat_axis=2, tiled=True)
        upper_panel, second_panel, from_sibling = neighbour_panels(own_panel)
        if k + 1 < chunks:
            _, parts[k + 1] = lax.optimization_barrier((from_sibling, parts[k + 1]))
        chunk_products.append(local_products(own_panel, [own_panel, upper_panel, second_panel]))
    band_limit = band_blocks[0]
    results = []
    for offset_index in range(BAND + 1):
        product = jnp.concatenate([p[offset_index] for p in chunk_products], axis=0)
        keep_flag = (offset_index <= band_limit).astype(jnp.bfloat16)
        results.append(product.astype(jnp.bfloat16) * keep_flag)
    return jnp.stack(results, axis=0)


def solution(mesh):
    in_specs = (P("freq", "chan"), P("freq"), P("chan"), P("chan"))
    out_specs = P(None, "freq", "chan", None)
    return jax.shard_map(shards, mesh=mesh, in_specs=in_specs, out_specs=out_specs, check_vma=False)
```

```python
import functools

import jax
import jax.numpy as jnp
from jax import lax
from jax.experimental import pallas as pl
from jax.experimental.pallas import tpu as pltpu
from jax.sharding import PartitionSpec as P

SEG_LEN = 256
BINS = 32
FIRST_BIN = 2
BAND = 2


EPS_POWER = 1e-06


def from_behind(block, axis, distance):
    devices = range(lax.axis_size(axis))
    route = [(i - distance, i) for i in devices if i - distance in devices]
    return lax.ppermute(block, axis, route)


def dft_table(seg_length, bin_count, first_bin):
    sample_index = jnp.arange(seg_length, dtype=jnp.int32)
    row_index = jnp.arange(2 * bin_count, dtype=jnp.int32)
    harmonic = row_index // 2 + first_bin
    phase_steps = harmonic[:, None] * sample_index[None, :] % seg_length
    phase_angle = 2.0 * jnp.pi / seg_length * phase_steps.astype(jnp.float32)
    hann_taper = 0.5 - 0.5 * jnp.cos(2.0 * jnp.pi / seg_length * sample_index.astype(jnp.float32))
    wave_rows = jnp.where(
        (row_index % 2 == 0)[:, None], jnp.cos(phase_angle), -jnp.sin(phase_angle)
    )
    return (hann_taper[None, :] * wave_rows).astype(jnp.bfloat16)


def spectra_kernel(seg_count, window, offs_ref, dft_ref, mask_ref, rec_hbm, out_ref, frames, sems):
    last_start = rec_hbm.shape[0] - window
    starts = []
    copies = []
    for j in range(seg_count):
        offset = offs_ref[j]
        start = pl.multiple_of(jnp.minimum((offset // 16) * 16, last_start), 16)
        starts.append(offset - start)
        copies.append(
            pltpu.make_async_copy(rec_hbm.at[pl.ds(start, window)], frames.at[j], sems.at[j])
        )
    for copy in copies:
        copy.start()
    dft = dft_ref[...]
    live = mask_ref[...]
    for j in range(seg_count):
        shifted = pltpu.roll(dft, starts[j], 1)[:, :window].astype(jnp.bfloat16)
        copies[j].wait()
        spec = jnp.dot(shifted, frames[j], preferred_element_type=jnp.float32)
        power = jnp.sum(spec * spec, axis=0, keepdims=True) * (1.0 / BINS)
        scale = live / jnp.sqrt(power + EPS_POWER)
        out_ref[j] = (spec * scale).astype(out_ref.dtype)


def whitened_spectra(records, offsets, dead_mask, dft_rows):
    seg_count = offsets.shape[0]
    channels = records.shape[1]
    window = SEG_LEN + 16
    rows = dft_rows.shape[0]
    padded = jnp.pad(dft_rows.astype(jnp.float32), ((0, 0), (0, 128)))
    live = dead_mask.astype(jnp.float32).reshape(1, channels)
    return pl.pallas_call(
        functools.partial(spectra_kernel, seg_count, window),
        out_shape=jax.ShapeDtypeStruct((seg_count, rows, channels), jnp.bfloat16),
        grid_spec=pltpu.PrefetchScalarGridSpec(
            num_scalar_prefetch=1,
            grid=(1,),
            in_specs=[
                pl.BlockSpec((rows, SEG_LEN + 128), lambda i, offs: (0, 0)),
                pl.BlockSpec((1, channels), lambda i, offs: (0, 0)),
                pl.BlockSpec(memory_space=pl.ANY),
            ],
            out_specs=pl.BlockSpec((seg_count, rows, channels), lambda i, offs: (0, 0, 0)),
            scratch_shapes=[
                pltpu.VMEM((seg_count, window, channels), records.dtype),
                pltpu.SemaphoreType.DMA((seg_count,)),
            ],
        ),
        compiler_params=pltpu.CompilerParams(vmem_limit_bytes=56 * 1024 * 1024),
        cost_estimate=pl.CostEstimate(
            flops=2 * seg_count * rows * window * channels,
            bytes_accessed=seg_count * (window + rows) * channels * 2,
            transcendentals=seg_count * channels,
        ),
    )(offsets, padded, live, records)


def local_products(left_panel, partner_panels):
    seg_count = left_panel.shape[2]
    results = []
    for right_panel in partner_panels:
        turned = jnp.stack([-right_panel[:, 1], right_panel[:, 0]], axis=1)
        both = jnp.concatenate([right_panel, turned], axis=3)
        product = jnp.einsum(
            "fpsi,fpsj->fij", left_panel, both, preferred_element_type=jnp.float32
        )
        results.append(product * (1.0 / seg_count))
    return results


def neighbour_panels(own_panel):
    n_chan = lax.axis_size("chan")
    second_panel = from_behind(own_panel, "chan", -2)
    from_sibling = lax.ppermute(own_panel, "chan", [(c + 1, c) for c in range(0, n_chan, 2)])
    from_forward = lax.ppermute(second_panel, "chan", [(c - 1, c) for c in range(1, n_chan, 2)])
    odd = lax.axis_index("chan") % 2 == 1
    upper_panel = jnp.where(odd, from_forward, from_sibling)
    return upper_panel, second_panel, from_sibling


def shards(records, offsets, dead_mask, band_blocks):
    n_freq = lax.axis_size("freq")
    per_device = BINS // n_freq
    chunks = 2
    per_chunk = per_device // chunks
    table = dft_table(SEG_LEN, BINS, FIRST_BIN).reshape(n_freq, chunks, per_chunk, 2, SEG_LEN)
    table = table.transpose(3, 1, 0, 2, 4).reshape(2 * BINS, SEG_LEN)
    per_segment = whitened_spectra(records, offsets, dead_mask, table)
    seg_count, rows, channels = per_segment.shape
    slabs = per_segment.reshape(seg_count, 2, chunks, n_freq * per_chunk, channels)
    parts = [slabs[:, :, k].transpose(2, 1, 0, 3) for k in range(chunks)]
    chunk_products = []
    for k in range(chunks):
        own_panel = lax.all_to_all(parts[k], "freq", split_axis=0, concat_axis=2, tiled=True)
        upper_panel, second_panel, from_sibling = neighbour_panels(own_panel)
        if k + 1 < chunks:
            _, parts[k + 1] = lax.optimization_barrier((from_sibling, parts[k + 1]))
        chunk_products.append(local_products(own_panel, [own_panel, upper_panel, second_panel]))
    band_limit = band_blocks[0]
    first = chunk_products[0][0]
    cross = jnp.zeros((BAND + 1, per_device) + first.shape[1:], jnp.bfloat16)
    for k, products in enumerate(chunk_products):
        for offset_index, product in enumerate(products):
            keep_flag = (offset_index <= band_limit).astype(jnp.bfloat16)
            block = (product.astype(jnp.bfloat16) * keep_flag)[None]
            cross = lax.dynamic_update_slice(cross, block, (offset_index, k * per_chunk, 0, 0))
    return cross


def solution(mesh):
    in_specs = (P("freq", "chan"), P("freq"), P("chan"), P("chan"))
    out_specs = P(None, "freq", "chan", None)
    return jax.shard_map(shards, mesh=mesh, in_specs=in_specs, out_specs=out_specs, check_vma=False)
```

```python
import functools

import jax
import jax.numpy as jnp
from jax import lax
from jax.experimental import pallas as pl
from jax.experimental.pallas import tpu as pltpu
from jax.sharding import PartitionSpec as P

SEG_LEN = 256
BINS = 32
FIRST_BIN = 2
BAND = 2


EPS_POWER = 1e-06


def from_behind(block, axis, distance):
    devices = range(lax.axis_size(axis))
    route = [(i - distance, i) for i in devices if i - distance in devices]
    return lax.ppermute(block, axis, route)


def dft_table(seg_length, bin_count, first_bin):
    sample_index = jnp.arange(seg_length, dtype=jnp.int32)
    row_index = jnp.arange(2 * bin_count, dtype=jnp.int32)
    harmonic = row_index // 2 + first_bin
    phase_steps = harmonic[:, None] * sample_index[None, :] % seg_length
    phase_angle = 2.0 * jnp.pi / seg_length * phase_steps.astype(jnp.float32)
    hann_taper = 0.5 - 0.5 * jnp.cos(2.0 * jnp.pi / seg_length * sample_index.astype(jnp.float32))
    wave_rows = jnp.where(
        (row_index % 2 == 0)[:, None], jnp.cos(phase_angle), -jnp.sin(phase_angle)
    )
    return (hann_taper[None, :] * wave_rows).astype(jnp.bfloat16)


def spectra_kernel(seg_count, window, offs_ref, dft_ref, mask_ref, rec_hbm, out_ref, frames, sems):
    last_start = rec_hbm.shape[0] - window
    starts = []
    copies = []
    for j in range(seg_count):
        offset = offs_ref[j]
        start = pl.multiple_of(jnp.minimum((offset // 16) * 16, last_start), 16)
        starts.append(offset - start)
        copies.append(
            pltpu.make_async_copy(rec_hbm.at[pl.ds(start, window)], frames.at[j], sems.at[j])
        )
    for copy in copies:
        copy.start()
    dft = dft_ref[...]
    live = mask_ref[...]
    for j in range(seg_count):
        shifted = pltpu.roll(dft, starts[j], 1)[:, :window].astype(jnp.bfloat16)
        copies[j].wait()
        spec = jnp.dot(shifted, frames[j], preferred_element_type=jnp.float32)
        power = jnp.sum(spec * spec, axis=0, keepdims=True) * (1.0 / BINS)
        scale = live / jnp.sqrt(power + EPS_POWER)
        out_ref[j] = (spec * scale).astype(out_ref.dtype)


def whitened_spectra(records, offsets, dead_mask, dft_rows):
    seg_count = offsets.shape[0]
    channels = records.shape[1]
    window = SEG_LEN + 16
    rows = dft_rows.shape[0]
    padded = jnp.pad(dft_rows.astype(jnp.float32), ((0, 0), (0, 128)))
    live = dead_mask.astype(jnp.float32).reshape(1, channels)
    return pl.pallas_call(
        functools.partial(spectra_kernel, seg_count, window),
        out_shape=jax.ShapeDtypeStruct((seg_count, rows, channels), jnp.bfloat16),
        grid_spec=pltpu.PrefetchScalarGridSpec(
            num_scalar_prefetch=1,
            grid=(1,),
            in_specs=[
                pl.BlockSpec((rows, SEG_LEN + 128), lambda i, offs: (0, 0)),
                pl.BlockSpec((1, channels), lambda i, offs: (0, 0)),
                pl.BlockSpec(memory_space=pl.ANY),
            ],
            out_specs=pl.BlockSpec((seg_count, rows, channels), lambda i, offs: (0, 0, 0)),
            scratch_shapes=[
                pltpu.VMEM((seg_count, window, channels), records.dtype),
                pltpu.SemaphoreType.DMA((seg_count,)),
            ],
        ),
        compiler_params=pltpu.CompilerParams(vmem_limit_bytes=56 * 1024 * 1024),
        cost_estimate=pl.CostEstimate(
            flops=2 * seg_count * rows * window * channels,
            bytes_accessed=seg_count * (window + rows) * channels * 2,
            transcendentals=seg_count * channels,
        ),
    )(offsets, padded, live, records)


def local_products(left_panel, partner_panels):
    seg_count = left_panel.shape[2]
    results = []
    for right_panel in partner_panels:
        turned = jnp.stack([-right_panel[:, 1], right_panel[:, 0]], axis=1)
        both = jnp.concatenate([right_panel, turned], axis=3)
        product = jnp.einsum(
            "fpsi,fpsj->fij", left_panel, both, preferred_element_type=jnp.float32
        )
        results.append(product * (1.0 / seg_count))
    return results


def neighbour_panels(own_panel):
    n_chan = lax.axis_size("chan")
    second_panel = from_behind(own_panel, "chan", -2)
    from_sibling = lax.ppermute(own_panel, "chan", [(c + 1, c) for c in range(0, n_chan, 2)])
    from_forward = lax.ppermute(second_panel, "chan", [(c - 1, c) for c in range(1, n_chan, 2)])
    odd = lax.axis_index("chan") % 2 == 1
    upper_panel = jnp.where(odd, from_forward, from_sibling)
    return upper_panel, second_panel, from_sibling


def shards(records, offsets, dead_mask, band_blocks):
    n_freq = lax.axis_size("freq")
    per_device = BINS // n_freq
    sizes = [2, 1, 1]
    chunks = len(sizes)
    bounds = [sum(sizes[:k]) for k in range(chunks + 1)]
    table = dft_table(SEG_LEN, BINS, FIRST_BIN).reshape(n_freq, per_device, 2, SEG_LEN)
    table = jnp.concatenate(
        [table[:, bounds[k]:bounds[k + 1]].reshape(n_freq * sizes[k], 2, SEG_LEN) for k in range(chunks)], axis=0
    )
    table = table.transpose(1, 0, 2).reshape(2 * BINS, SEG_LEN)
    per_segment = whitened_spectra(records, offsets, dead_mask, table)
    seg_count, rows, channels = per_segment.shape
    slabs = per_segment.reshape(seg_count, 2, BINS, channels)
    parts = [
        slabs[:, :, n_freq * bounds[k]:n_freq * bounds[k + 1]].transpose(2, 1, 0, 3) for k in range(chunks)
    ]
    chunk_products = []
    for k in range(chunks):
        own_panel = lax.all_to_all(parts[k], "freq", split_axis=0, concat_axis=2, tiled=True)
        upper_panel, second_panel, from_sibling = neighbour_panels(own_panel)
        if k + 1 < chunks:
            _, parts[k + 1] = lax.optimization_barrier((from_sibling, parts[k + 1]))
        chunk_products.append(local_products(own_panel, [own_panel, upper_panel, second_panel]))
    band_limit = band_blocks[0]
    results = []
    for offset_index in range(BAND + 1):
        product = jnp.concatenate([p[offset_index] for p in chunk_products], axis=0)
        keep_flag = (offset_index <= band_limit).astype(jnp.bfloat16)
        results.append(product.astype(jnp.bfloat16) * keep_flag)
    return jnp.stack(results, axis=0)


def solution(mesh):
    in_specs = (P("freq", "chan"), P("freq"), P("chan"), P("chan"))
    out_specs = P(None, "freq", "chan", None)
    return jax.shard_map(shards, mesh=mesh, in_specs=in_specs, out_specs=out_specs, check_vma=False)
```

```python
import functools

import jax
import jax.numpy as jnp
from jax import lax
from jax.experimental import pallas as pl
from jax.experimental.pallas import tpu as pltpu
from jax.sharding import PartitionSpec as P

SEG_LEN = 256
BINS = 32
FIRST_BIN = 2
BAND = 2


EPS_POWER = 1e-06


def from_behind(block, axis, distance):
    devices = range(lax.axis_size(axis))
    route = [(i - distance, i) for i in devices if i - distance in devices]
    return lax.ppermute(block, axis, route)


def dft_table(seg_length, bin_count, first_bin):
    sample_index = jnp.arange(seg_length, dtype=jnp.int32)
    row_index = jnp.arange(2 * bin_count, dtype=jnp.int32)
    harmonic = row_index // 2 + first_bin
    phase_steps = harmonic[:, None] * sample_index[None, :] % seg_length
    phase_angle = 2.0 * jnp.pi / seg_length * phase_steps.astype(jnp.float32)
    hann_taper = 0.5 - 0.5 * jnp.cos(2.0 * jnp.pi / seg_length * sample_index.astype(jnp.float32))
    wave_rows = jnp.where(
        (row_index % 2 == 0)[:, None], jnp.cos(phase_angle), -jnp.sin(phase_angle)
    )
    return (hann_taper[None, :] * wave_rows).astype(jnp.bfloat16)


def spectra_kernel(seg_count, window, offs_ref, dft_ref, mask_ref, rec_hbm, out_ref, frames, sems):
    last_start = rec_hbm.shape[0] - window
    starts = []
    copies = []
    for j in range(seg_count):
        offset = offs_ref[j]
        start = pl.multiple_of(jnp.minimum((offset // 16) * 16, last_start), 16)
        starts.append(offset - start)
        copies.append(
            pltpu.make_async_copy(rec_hbm.at[pl.ds(start, window)], frames.at[j], sems.at[j])
        )
    for copy in copies:
        copy.start()
    dft = dft_ref[...]
    live = mask_ref[...]
    for j in range(seg_count):
        shifted = pltpu.roll(dft, starts[j], 1)[:, :window].astype(jnp.bfloat16)
        copies[j].wait()
        spec = jnp.dot(shifted, frames[j], preferred_element_type=jnp.float32)
        power = jnp.sum(spec * spec, axis=0, keepdims=True) * (1.0 / BINS)
        scale = live / jnp.sqrt(power + EPS_POWER)
        out_ref[j] = (spec * scale).astype(out_ref.dtype)


def whitened_spectra(records, offsets, dead_mask, dft_rows):
    seg_count = offsets.shape[0]
    channels = records.shape[1]
    window = SEG_LEN + 16
    rows = dft_rows.shape[0]
    padded = jnp.pad(dft_rows.astype(jnp.float32), ((0, 0), (0, 128)))
    live = dead_mask.astype(jnp.float32).reshape(1, channels)
    return pl.pallas_call(
        functools.partial(spectra_kernel, seg_count, window),
        out_shape=jax.ShapeDtypeStruct((seg_count, rows, channels), jnp.bfloat16),
        grid_spec=pltpu.PrefetchScalarGridSpec(
            num_scalar_prefetch=1,
            grid=(1,),
            in_specs=[
                pl.BlockSpec((rows, SEG_LEN + 128), lambda i, offs: (0, 0)),
                pl.BlockSpec((1, channels), lambda i, offs: (0, 0)),
                pl.BlockSpec(memory_space=pl.ANY),
            ],
            out_specs=pl.BlockSpec((seg_count, rows, channels), lambda i, offs: (0, 0, 0)),
            scratch_shapes=[
                pltpu.VMEM((seg_count, window, channels), records.dtype),
                pltpu.SemaphoreType.DMA((seg_count,)),
            ],
        ),
        compiler_params=pltpu.CompilerParams(vmem_limit_bytes=56 * 1024 * 1024),
        cost_estimate=pl.CostEstimate(
            flops=2 * seg_count * rows * window * channels,
            bytes_accessed=seg_count * (window + rows) * channels * 2,
            transcendentals=seg_count * channels,
        ),
    )(offsets, padded, live, records)


def local_products(left_panel, partner_panels):
    seg_count = left_panel.shape[2]
    results = []
    for right_panel in partner_panels:
        turned = jnp.stack([-right_panel[:, 1], right_panel[:, 0]], axis=1)
        both = jnp.concatenate([right_panel, turned], axis=3)
        product = jnp.einsum(
            "fpsi,fpsj->fij", left_panel, both, preferred_element_type=jnp.float32
        )
        results.append(product * (1.0 / seg_count))
    return results


def neighbour_panels(own_panel, merged=False):
    n_chan = lax.axis_size("chan")
    second_panel = from_behind(own_panel, "chan", -2)
    odd = lax.axis_index("chan") % 2 == 1
    if merged:
        outgoing = jnp.where(odd, own_panel, second_panel)
        pairs = [(c, c - 1) for c in range(1, n_chan, 2)] + [(c, c + 1) for c in range(0, n_chan - 1, 2)]
        upper_panel = lax.ppermute(outgoing, "chan", pairs)
        return upper_panel, second_panel, upper_panel
    from_sibling = lax.ppermute(own_panel, "chan", [(c + 1, c) for c in range(0, n_chan, 2)])
    from_forward = lax.ppermute(second_panel, "chan", [(c - 1, c) for c in range(1, n_chan, 2)])
    odd = lax.axis_index("chan") % 2 == 1
    upper_panel = jnp.where(odd, from_forward, from_sibling)
    return upper_panel, second_panel, from_sibling


def shards(records, offsets, dead_mask, band_blocks):
    n_freq = lax.axis_size("freq")
    per_device = BINS // n_freq
    chunks = 2
    per_chunk = per_device // chunks
    table = dft_table(SEG_LEN, BINS, FIRST_BIN).reshape(n_freq, chunks, per_chunk, 2, SEG_LEN)
    table = table.transpose(3, 1, 0, 2, 4).reshape(2 * BINS, SEG_LEN)
    per_segment = whitened_spectra(records, offsets, dead_mask, table)
    seg_count, rows, channels = per_segment.shape
    slabs = per_segment.reshape(seg_count, 2, chunks, n_freq * per_chunk, channels)
    parts = [slabs[:, :, k].transpose(2, 1, 0, 3) for k in range(chunks)]
    chunk_products = []
    for k in range(chunks):
        own_panel = lax.all_to_all(parts[k], "freq", split_axis=0, concat_axis=2, tiled=True)
        upper_panel, second_panel, from_sibling = neighbour_panels(own_panel, merged=k + 1 == chunks)
        if k + 1 < chunks:
            _, parts[k + 1] = lax.optimization_barrier((from_sibling, parts[k + 1]))
        chunk_products.append(local_products(own_panel, [own_panel, upper_panel, second_panel]))
    band_limit = band_blocks[0]
    results = []
    for offset_index in range(BAND + 1):
        product = jnp.concatenate([p[offset_index] for p in chunk_products], axis=0)
        keep_flag = (offset_index <= band_limit).astype(jnp.bfloat16)
        results.append(product.astype(jnp.bfloat16) * keep_flag)
    return jnp.stack(results, axis=0)


def solution(mesh):
    in_specs = (P("freq", "chan"), P("freq"), P("chan"), P("chan"))
    out_specs = P(None, "freq", "chan", None)
    return jax.shard_map(shards, mesh=mesh, in_specs=in_specs, out_specs=out_specs, check_vma=False)
```

```python
import functools

import jax
import jax.numpy as jnp
from jax import lax
from jax.experimental import pallas as pl
from jax.experimental.pallas import tpu as pltpu
from jax.sharding import PartitionSpec as P

SEG_LEN = 256
BINS = 32
FIRST_BIN = 2
BAND = 2


EPS_POWER = 1e-06


def from_behind(block, axis, distance):
    devices = range(lax.axis_size(axis))
    route = [(i - distance, i) for i in devices if i - distance in devices]
    return lax.ppermute(block, axis, route)


def dft_table(seg_length, bin_count, first_bin):
    sample_index = jnp.arange(seg_length, dtype=jnp.int32)
    row_index = jnp.arange(2 * bin_count, dtype=jnp.int32)
    harmonic = row_index // 2 + first_bin
    phase_steps = harmonic[:, None] * sample_index[None, :] % seg_length
    phase_angle = 2.0 * jnp.pi / seg_length * phase_steps.astype(jnp.float32)
    hann_taper = 0.5 - 0.5 * jnp.cos(2.0 * jnp.pi / seg_length * sample_index.astype(jnp.float32))
    wave_rows = jnp.where(
        (row_index % 2 == 0)[:, None], jnp.cos(phase_angle), -jnp.sin(phase_angle)
    )
    return (hann_taper[None, :] * wave_rows).astype(jnp.bfloat16)


def spectra_kernel(seg_count, window, chunks, offs_ref, dft_ref, mask_ref, rec_hbm, *refs):
    out_refs, (frames, sems) = refs[:chunks], refs[chunks:]
    last_start = rec_hbm.shape[0] - window
    starts = []
    copies = []
    for j in range(seg_count):
        offset = offs_ref[j]
        start = pl.multiple_of(jnp.minimum((offset // 16) * 16, last_start), 16)
        starts.append(offset - start)
        copies.append(
            pltpu.make_async_copy(rec_hbm.at[pl.ds(start, window)], frames.at[j], sems.at[j])
        )
    for copy in copies:
        copy.start()
    dft = dft_ref[...]
    live = mask_ref[...]
    for j in range(seg_count):
        shifted = pltpu.roll(dft, starts[j], 1)[:, :window].astype(jnp.bfloat16)
        copies[j].wait()
        spec = jnp.dot(shifted, frames[j], preferred_element_type=jnp.float32)
        power = jnp.sum(spec * spec, axis=0, keepdims=True) * (1.0 / BINS)
        scale = live / jnp.sqrt(power + EPS_POWER)
        white = (spec * scale).astype(jnp.bfloat16)
        slab = white.shape[0] // (2 * chunks)
        for k, out_ref in enumerate(out_refs):
            for part in range(2):
                first = (part * chunks + k) * slab
                out_ref[j, part] = white[first:first + slab]


def whitened_spectra(records, offsets, dead_mask, dft_rows, chunks):
    seg_count = offsets.shape[0]
    channels = records.shape[1]
    window = SEG_LEN + 16
    rows = dft_rows.shape[0]
    padded = jnp.pad(dft_rows.astype(jnp.float32), ((0, 0), (0, 128)))
    live = dead_mask.astype(jnp.float32).reshape(1, channels)
    return pl.pallas_call(
        functools.partial(spectra_kernel, seg_count, window, chunks),
        out_shape=[
            jax.ShapeDtypeStruct((seg_count, 2, rows // (2 * chunks), channels), jnp.bfloat16)
            for _ in range(chunks)
        ],
        grid_spec=pltpu.PrefetchScalarGridSpec(
            num_scalar_prefetch=1,
            grid=(1,),
            in_specs=[
                pl.BlockSpec((rows, SEG_LEN + 128), lambda i, offs: (0, 0)),
                pl.BlockSpec((1, channels), lambda i, offs: (0, 0)),
                pl.BlockSpec(memory_space=pl.ANY),
            ],
            out_specs=[
                pl.BlockSpec((seg_count, 2, rows // (2 * chunks), channels), lambda i, offs: (0, 0, 0, 0))
                for _ in range(chunks)
            ],
            scratch_shapes=[
                pltpu.VMEM((seg_count, window, channels), records.dtype),
                pltpu.SemaphoreType.DMA((seg_count,)),
            ],
        ),
        compiler_params=pltpu.CompilerParams(vmem_limit_bytes=56 * 1024 * 1024),
        cost_estimate=pl.CostEstimate(
            flops=2 * seg_count * rows * window * channels,
            bytes_accessed=seg_count * (window + rows) * channels * 2,
            transcendentals=seg_count * channels,
        ),
    )(offsets, padded, live, records)


def local_products(left_panel, partner_panels):
    seg_count = left_panel.shape[2]
    results = []
    for right_panel in partner_panels:
        turned = jnp.stack([-right_panel[:, 1], right_panel[:, 0]], axis=1)
        both = jnp.concatenate([right_panel, turned], axis=3)
        product = jnp.einsum(
            "fpsi,fpsj->fij", left_panel, both, preferred_element_type=jnp.float32
        )
        results.append(product * (1.0 / seg_count))
    return results


def neighbour_panels(own_panel, merged=False):
    n_chan = lax.axis_size("chan")
    second_panel = from_behind(own_panel, "chan", -2)
    odd = lax.axis_index("chan") % 2 == 1
    if merged:
        outgoing = jnp.where(odd, own_panel, second_panel)
        pairs = [(c, c - 1) for c in range(1, n_chan, 2)] + [(c, c + 1) for c in range(0, n_chan - 1, 2)]
        upper_panel = lax.ppermute(outgoing, "chan", pairs)
        return upper_panel, second_panel, upper_panel
    from_sibling = lax.ppermute(own_panel, "chan", [(c + 1, c) for c in range(0, n_chan, 2)])
    from_forward = lax.ppermute(second_panel, "chan", [(c - 1, c) for c in range(1, n_chan, 2)])
    odd = lax.axis_index("chan") % 2 == 1
    upper_panel = jnp.where(odd, from_forward, from_sibling)
    return upper_panel, second_panel, from_sibling


def shards(records, offsets, dead_mask, band_blocks):
    n_freq = lax.axis_size("freq")
    per_device = BINS // n_freq
    chunks = 2
    per_chunk = per_device // chunks
    table = dft_table(SEG_LEN, BINS, FIRST_BIN).reshape(n_freq, chunks, per_chunk, 2, SEG_LEN)
    table = table.transpose(3, 1, 0, 2, 4).reshape(2 * BINS, SEG_LEN)
    slabs = whitened_spectra(records, offsets, dead_mask, table, chunks)
    seg_count, _, _, channels = slabs[0].shape
    parts = [slab.transpose(2, 1, 0, 3) for slab in slabs]
    chunk_products = []
    for k in range(chunks):
        own_panel = lax.all_to_all(parts[k], "freq", split_axis=0, concat_axis=2, tiled=True)
        upper_panel, second_panel, from_sibling = neighbour_panels(own_panel, merged=k + 1 == chunks)
        if k + 1 < chunks:
            _, parts[k + 1] = lax.optimization_barrier((from_sibling, parts[k + 1]))
        chunk_products.append(local_products(own_panel, [own_panel, upper_panel, second_panel]))
    band_limit = band_blocks[0]
    results = []
    for offset_index in range(BAND + 1):
        product = jnp.concatenate([p[offset_index] for p in chunk_products], axis=0)
        keep_flag = (offset_index <= band_limit).astype(jnp.bfloat16)
        results.append(product.astype(jnp.bfloat16) * keep_flag)
    return jnp.stack(results, axis=0)


def solution(mesh):
    in_specs = (P("freq", "chan"), P("freq"), P("chan"), P("chan"))
    out_specs = P(None, "freq", "chan", None)
    return jax.shard_map(shards, mesh=mesh, in_specs=in_specs, out_specs=out_specs, check_vma=False)
```

```python
import functools

import jax
import jax.numpy as jnp
from jax import lax
from jax.experimental import pallas as pl
from jax.experimental.pallas import tpu as pltpu
from jax.sharding import PartitionSpec as P

SEG_LEN = 256
BINS = 32
FIRST_BIN = 2
BAND = 2


EPS_POWER = 1e-06


def from_behind(block, axis, distance):
    devices = range(lax.axis_size(axis))
    route = [(i - distance, i) for i in devices if i - distance in devices]
    return lax.ppermute(block, axis, route)


def dft_table(seg_length, bin_count, first_bin):
    sample_index = jnp.arange(seg_length, dtype=jnp.int32)
    row_index = jnp.arange(2 * bin_count, dtype=jnp.int32)
    harmonic = row_index // 2 + first_bin
    phase_steps = harmonic[:, None] * sample_index[None, :] % seg_length
    phase_angle = 2.0 * jnp.pi / seg_length * phase_steps.astype(jnp.float32)
    hann_taper = 0.5 - 0.5 * jnp.cos(2.0 * jnp.pi / seg_length * sample_index.astype(jnp.float32))
    wave_rows = jnp.where(
        (row_index % 2 == 0)[:, None], jnp.cos(phase_angle), -jnp.sin(phase_angle)
    )
    return (hann_taper[None, :] * wave_rows).astype(jnp.bfloat16)


def spectra_kernel(seg_count, window, offs_ref, dft_ref, mask_ref, rec_hbm, out_ref, frames, sems):
    last_start = rec_hbm.shape[0] - window
    starts = []
    copies = []
    for j in range(seg_count):
        offset = offs_ref[j]
        start = pl.multiple_of(jnp.minimum((offset // 16) * 16, last_start), 16)
        starts.append(offset - start)
        copies.append(
            pltpu.make_async_copy(rec_hbm.at[pl.ds(start, window)], frames.at[j], sems.at[j])
        )
    for copy in copies:
        copy.start()
    dft = dft_ref[...]
    live = mask_ref[...]
    for j in range(seg_count):
        shifted = pltpu.roll(dft, starts[j], 1)[:, :window].astype(jnp.bfloat16)
        copies[j].wait()
        spec = jnp.dot(shifted, frames[j], preferred_element_type=jnp.float32)
        power = jnp.sum(spec * spec, axis=0, keepdims=True) * (1.0 / BINS)
        scale = live / jnp.sqrt(power + EPS_POWER)
        out_ref[j] = (spec * scale).astype(out_ref.dtype)


def whitened_spectra(records, offsets, dead_mask, dft_rows):
    seg_count = offsets.shape[0]
    channels = records.shape[1]
    window = SEG_LEN + 16
    rows = dft_rows.shape[0]
    padded = jnp.pad(dft_rows.astype(jnp.float32), ((0, 0), (0, 128)))
    live = dead_mask.astype(jnp.float32).reshape(1, channels)
    return pl.pallas_call(
        functools.partial(spectra_kernel, seg_count, window),
        out_shape=jax.ShapeDtypeStruct((seg_count, rows, channels), jnp.bfloat16),
        grid_spec=pltpu.PrefetchScalarGridSpec(
            num_scalar_prefetch=1,
            grid=(1,),
            in_specs=[
                pl.BlockSpec((rows, SEG_LEN + 128), lambda i, offs: (0, 0)),
                pl.BlockSpec((1, channels), lambda i, offs: (0, 0)),
                pl.BlockSpec(memory_space=pl.ANY),
            ],
            out_specs=pl.BlockSpec((seg_count, rows, channels), lambda i, offs: (0, 0, 0)),
            scratch_shapes=[
                pltpu.VMEM((seg_count, window, channels), records.dtype),
                pltpu.SemaphoreType.DMA((seg_count,)),
            ],
        ),
        compiler_params=pltpu.CompilerParams(vmem_limit_bytes=56 * 1024 * 1024),
        cost_estimate=pl.CostEstimate(
            flops=2 * seg_count * rows * window * channels,
            bytes_accessed=seg_count * (window + rows) * channels * 2,
            transcendentals=seg_count * channels,
        ),
    )(offsets, padded, live, records)


def local_products(left_panel, partner_panels):
    seg_count = left_panel.shape[2]
    turned = jnp.stack([left_panel[:, 1], -left_panel[:, 0]], axis=1)
    results = []
    for right_panel in partner_panels:
        real_part = jnp.einsum("fpsi,fpsj->fij", left_panel, right_panel, preferred_element_type=jnp.float32)
        imag_part = jnp.einsum("fpsi,fpsj->fij", turned, right_panel, preferred_element_type=jnp.float32)
        results.append(jnp.concatenate([real_part, imag_part], axis=2) * (1.0 / seg_count))
    return results


def neighbour_panels(own_panel, merged=False):
    n_chan = lax.axis_size("chan")
    second_panel = from_behind(own_panel, "chan", -2)
    odd = lax.axis_index("chan") % 2 == 1
    if merged:
        outgoing = jnp.where(odd, own_panel, second_panel)
        pairs = [(c, c - 1) for c in range(1, n_chan, 2)] + [(c, c + 1) for c in range(0, n_chan - 1, 2)]
        upper_panel = lax.ppermute(outgoing, "chan", pairs)
        return upper_panel, second_panel, upper_panel
    from_sibling = lax.ppermute(own_panel, "chan", [(c + 1, c) for c in range(0, n_chan, 2)])
    from_forward = lax.ppermute(second_panel, "chan", [(c - 1, c) for c in range(1, n_chan, 2)])
    odd = lax.axis_index("chan") % 2 == 1
    upper_panel = jnp.where(odd, from_forward, from_sibling)
    return upper_panel, second_panel, from_sibling


def shards(records, offsets, dead_mask, band_blocks):
    n_freq = lax.axis_size("freq")
    per_device = BINS // n_freq
    chunks = 2
    per_chunk = per_device // chunks
    table = dft_table(SEG_LEN, BINS, FIRST_BIN).reshape(n_freq, chunks, per_chunk, 2, SEG_LEN)
    table = table.transpose(3, 1, 0, 2, 4).reshape(2 * BINS, SEG_LEN)
    per_segment = whitened_spectra(records, offsets, dead_mask, table)
    seg_count, rows, channels = per_segment.shape
    slabs = per_segment.reshape(seg_count, 2, chunks, n_freq * per_chunk, channels)
    parts = [slabs[:, :, k].transpose(2, 1, 0, 3) for k in range(chunks)]
    chunk_products = []
    for k in range(chunks):
        own_panel = lax.all_to_all(parts[k], "freq", split_axis=0, concat_axis=2, tiled=True)
        upper_panel, second_panel, from_sibling = neighbour_panels(own_panel, merged=k + 1 == chunks)
        if k + 1 < chunks:
            _, parts[k + 1] = lax.optimization_barrier((from_sibling, parts[k + 1]))
        chunk_products.append(local_products(own_panel, [own_panel, upper_panel, second_panel]))
    band_limit = band_blocks[0]
    results = []
    for offset_index in range(BAND + 1):
        product = jnp.concatenate([p[offset_index] for p in chunk_products], axis=0)
        keep_flag = (offset_index <= band_limit).astype(jnp.bfloat16)
        results.append(product.astype(jnp.bfloat16) * keep_flag)
    return jnp.stack(results, axis=0)


def solution(mesh):
    in_specs = (P("freq", "chan"), P("freq"), P("chan"), P("chan"))
    out_specs = P(None, "freq", "chan", None)
    return jax.shard_map(shards, mesh=mesh, in_specs=in_specs, out_specs=out_specs, check_vma=False)
```

```python
import functools

import jax
import jax.numpy as jnp
from jax import lax
from jax.experimental import pallas as pl
from jax.experimental.pallas import tpu as pltpu
from jax.sharding import PartitionSpec as P

SEG_LEN = 256
BINS = 32
FIRST_BIN = 2
BAND = 2


EPS_POWER = 1e-06


def from_behind(block, axis, distance):
    devices = range(lax.axis_size(axis))
    route = [(i - distance, i) for i in devices if i - distance in devices]
    return lax.ppermute(block, axis, route)


def dft_table(seg_length, bin_count, first_bin):
    sample_index = jnp.arange(seg_length, dtype=jnp.int32)
    row_index = jnp.arange(2 * bin_count, dtype=jnp.int32)
    harmonic = row_index // 2 + first_bin
    phase_steps = harmonic[:, None] * sample_index[None, :] % seg_length
    phase_angle = 2.0 * jnp.pi / seg_length * phase_steps.astype(jnp.float32)
    hann_taper = 0.5 - 0.5 * jnp.cos(2.0 * jnp.pi / seg_length * sample_index.astype(jnp.float32))
    wave_rows = jnp.where(
        (row_index % 2 == 0)[:, None], jnp.cos(phase_angle), -jnp.sin(phase_angle)
    )
    return (hann_taper[None, :] * wave_rows).astype(jnp.bfloat16)


def spectra_kernel(seg_count, window, offs_ref, dft_ref, mask_ref, rec_hbm, out_ref, frames, sems):
    last_start = rec_hbm.shape[0] - window
    starts = []
    copies = []
    for j in range(seg_count):
        offset = offs_ref[j]
        start = pl.multiple_of(jnp.minimum((offset // 16) * 16, last_start), 16)
        starts.append(offset - start)
        copies.append(
            pltpu.make_async_copy(rec_hbm.at[pl.ds(start, window)], frames.at[j], sems.at[j])
        )
    for copy in copies:
        copy.start()
    dft = dft_ref[...]
    live = mask_ref[...]
    for j in range(seg_count):
        shifted = pltpu.roll(dft, starts[j], 1)[:, :window].astype(jnp.bfloat16)
        copies[j].wait()
        spec = jnp.dot(shifted, frames[j], preferred_element_type=jnp.float32)
        power = jnp.sum(spec * spec, axis=0, keepdims=True) * (1.0 / BINS)
        scale = live / jnp.sqrt(power + EPS_POWER)
        out_ref[j] = (spec * scale).astype(out_ref.dtype)


def whitened_spectra(records, offsets, dead_mask, dft_rows):
    seg_count = offsets.shape[0]
    channels = records.shape[1]
    window = SEG_LEN + 16
    rows = dft_rows.shape[0]
    padded = jnp.pad(dft_rows.astype(jnp.float32), ((0, 0), (0, 128)))
    live = dead_mask.astype(jnp.float32).reshape(1, channels)
    return pl.pallas_call(
        functools.partial(spectra_kernel, seg_count, window),
        out_shape=jax.ShapeDtypeStruct((seg_count, rows, channels), jnp.bfloat16),
        grid_spec=pltpu.PrefetchScalarGridSpec(
            num_scalar_prefetch=1,
            grid=(1,),
            in_specs=[
                pl.BlockSpec((rows, SEG_LEN + 128), lambda i, offs: (0, 0)),
                pl.BlockSpec((1, channels), lambda i, offs: (0, 0)),
                pl.BlockSpec(memory_space=pl.ANY),
            ],
            out_specs=pl.BlockSpec((seg_count, rows, channels), lambda i, offs: (0, 0, 0)),
            scratch_shapes=[
                pltpu.VMEM((seg_count, window, channels), records.dtype),
                pltpu.SemaphoreType.DMA((seg_count,)),
            ],
        ),
        compiler_params=pltpu.CompilerParams(vmem_limit_bytes=56 * 1024 * 1024),
        cost_estimate=pl.CostEstimate(
            flops=2 * seg_count * rows * window * channels,
            bytes_accessed=seg_count * (window + rows) * channels * 2,
            transcendentals=seg_count * channels,
        ),
    )(offsets, padded, live, records)


def local_products(left_panel, partner_panels):
    seg_count = left_panel.shape[2]
    results = []
    for right_panel in partner_panels:
        turned = jnp.stack([-right_panel[:, 1], right_panel[:, 0]], axis=1)
        both = jnp.concatenate([right_panel, turned], axis=3)
        product = jnp.einsum(
            "fpsi,fpsj->fij", left_panel, both, preferred_element_type=jnp.float32
        )
        results.append(product * (1.0 / seg_count))
    return results


def neighbour_panels(own_panel, merged=False):
    n_chan = lax.axis_size("chan")
    second_panel = from_behind(own_panel, "chan", -2)
    odd = lax.axis_index("chan") % 2 == 1
    if merged:
        outgoing = jnp.where(odd, own_panel, second_panel)
        pairs = [(c, c - 1) for c in range(1, n_chan, 2)] + [(c, c + 1) for c in range(0, n_chan - 1, 2)]
        upper_panel = lax.ppermute(outgoing, "chan", pairs)
        return upper_panel, second_panel, upper_panel
    from_sibling = lax.ppermute(own_panel, "chan", [(c + 1, c) for c in range(0, n_chan, 2)])
    from_forward = lax.ppermute(second_panel, "chan", [(c - 1, c) for c in range(1, n_chan, 2)])
    odd = lax.axis_index("chan") % 2 == 1
    upper_panel = jnp.where(odd, from_forward, from_sibling)
    return upper_panel, second_panel, from_sibling


def shards(records, offsets, dead_mask, band_blocks):
    n_freq = lax.axis_size("freq")
    per_device = BINS // n_freq
    chunks = 2
    per_chunk = per_device // chunks
    table = dft_table(SEG_LEN, BINS, FIRST_BIN).reshape(n_freq, chunks, per_chunk, 2, SEG_LEN)
    table = table.transpose(3, 1, 0, 2, 4).reshape(2 * BINS, SEG_LEN)
    per_segment = whitened_spectra(records, offsets, dead_mask, table)
    seg_count, rows, channels = per_segment.shape
    slabs = per_segment.reshape(seg_count, 2, chunks, n_freq * per_chunk, channels)
    parts = [slabs[:, :, k].transpose(2, 1, 0, 3) for k in range(chunks)]
    chunk_products = []
    for k in range(chunks):
        own_panel = lax.all_to_all(parts[k], "freq", split_axis=0, concat_axis=2, tiled=True)
        upper_panel, second_panel, _ = neighbour_panels(own_panel, merged=True)
        if k + 1 < chunks:
            _, parts[k + 1] = lax.optimization_barrier((own_panel, parts[k + 1]))
        chunk_products.append(local_products(own_panel, [own_panel, upper_panel, second_panel]))
    band_limit = band_blocks[0]
    results = []
    for offset_index in range(BAND + 1):
        product = jnp.concatenate([p[offset_index] for p in chunk_products], axis=0)
        keep_flag = (offset_index <= band_limit).astype(jnp.bfloat16)
        results.append(product.astype(jnp.bfloat16) * keep_flag)
    return jnp.stack(results, axis=0)


def solution(mesh):
    in_specs = (P("freq", "chan"), P("freq"), P("chan"), P("chan"))
    out_specs = P(None, "freq", "chan", None)
    return jax.shard_map(shards, mesh=mesh, in_specs=in_specs, out_specs=out_specs, check_vma=False)
```

```python
import functools

import jax
import jax.numpy as jnp
from jax import lax
from jax.experimental import pallas as pl
from jax.experimental.pallas import tpu as pltpu
from jax.sharding import PartitionSpec as P

SEG_LEN = 256
BINS = 32
FIRST_BIN = 2
BAND = 2


EPS_POWER = 1e-06


def from_behind(block, axis, distance):
    devices = range(lax.axis_size(axis))
    route = [(i - distance, i) for i in devices if i - distance in devices]
    return lax.ppermute(block, axis, route)


def dft_table(seg_length, bin_count, first_bin):
    sample_index = jnp.arange(seg_length, dtype=jnp.int32)
    row_index = jnp.arange(2 * bin_count, dtype=jnp.int32)
    harmonic = row_index // 2 + first_bin
    phase_steps = harmonic[:, None] * sample_index[None, :] % seg_length
    phase_angle = 2.0 * jnp.pi / seg_length * phase_steps.astype(jnp.float32)
    hann_taper = 0.5 - 0.5 * jnp.cos(2.0 * jnp.pi / seg_length * sample_index.astype(jnp.float32))
    wave_rows = jnp.where(
        (row_index % 2 == 0)[:, None], jnp.cos(phase_angle), -jnp.sin(phase_angle)
    )
    return (hann_taper[None, :] * wave_rows).astype(jnp.bfloat16)


def spectra_kernel(seg_count, window, offs_ref, dft_ref, mask_ref, rec_hbm, out_ref, frames, sems):
    last_start = rec_hbm.shape[0] - window
    starts = []
    copies = []
    for j in range(seg_count):
        offset = offs_ref[j]
        start = pl.multiple_of(jnp.minimum((offset // 16) * 16, last_start), 16)
        starts.append(offset - start)
        copies.append(
            pltpu.make_async_copy(rec_hbm.at[pl.ds(start, window)], frames.at[j], sems.at[j])
        )
    for copy in copies:
        copy.start()
    dft = dft_ref[...]
    live = mask_ref[...]
    for j in range(seg_count):
        shifted = pltpu.roll(dft, starts[j], 1)[:, :window].astype(jnp.bfloat16)
        copies[j].wait()
        spec = jnp.dot(shifted, frames[j], preferred_element_type=jnp.float32)
        power = jnp.sum(spec * spec, axis=0, keepdims=True) * (1.0 / BINS)
        scale = live / jnp.sqrt(power + EPS_POWER)
        out_ref[j] = (spec * scale).astype(out_ref.dtype)


def whitened_spectra(records, offsets, dead_mask, dft_rows):
    seg_count = offsets.shape[0]
    channels = records.shape[1]
    window = SEG_LEN + 16
    rows = dft_rows.shape[0]
    padded = jnp.pad(dft_rows.astype(jnp.float32), ((0, 0), (0, 128)))
    live = dead_mask.astype(jnp.float32).reshape(1, channels)
    return pl.pallas_call(
        functools.partial(spectra_kernel, seg_count, window),
        out_shape=jax.ShapeDtypeStruct((seg_count, rows, channels), jnp.bfloat16),
        grid_spec=pltpu.PrefetchScalarGridSpec(
            num_scalar_prefetch=1,
            grid=(1,),
            in_specs=[
                pl.BlockSpec((rows, SEG_LEN + 128), lambda i, offs: (0, 0)),
                pl.BlockSpec((1, channels), lambda i, offs: (0, 0)),
                pl.BlockSpec(memory_space=pl.ANY),
            ],
            out_specs=pl.BlockSpec((seg_count, rows, channels), lambda i, offs: (0, 0, 0)),
            scratch_shapes=[
                pltpu.VMEM((seg_count, window, channels), records.dtype),
                pltpu.SemaphoreType.DMA((seg_count,)),
            ],
        ),
        compiler_params=pltpu.CompilerParams(vmem_limit_bytes=32 * 1024 * 1024),
        cost_estimate=pl.CostEstimate(
            flops=2 * seg_count * rows * window * channels,
            bytes_accessed=seg_count * (window + rows) * channels * 2,
            transcendentals=seg_count * channels,
        ),
    )(offsets, padded, live, records)


def local_products(left_panel, partner_panels):
    seg_count = left_panel.shape[2]
    results = []
    for right_panel in partner_panels:
        turned = jnp.stack([-right_panel[:, 1], right_panel[:, 0]], axis=1)
        both = jnp.concatenate([right_panel, turned], axis=3)
        product = jnp.einsum(
            "fpsi,fpsj->fij", left_panel, both, preferred_element_type=jnp.float32
        )
        results.append(product * (1.0 / seg_count))
    return results


def neighbour_panels(own_panel, merged=False):
    n_chan = lax.axis_size("chan")
    second_panel = from_behind(own_panel, "chan", -2)
    odd = lax.axis_index("chan") % 2 == 1
    if merged:
        outgoing = jnp.where(odd, own_panel, second_panel)
        pairs = [(c, c - 1) for c in range(1, n_chan, 2)] + [(c, c + 1) for c in range(0, n_chan - 1, 2)]
        upper_panel = lax.ppermute(outgoing, "chan", pairs)
        return upper_panel, second_panel, upper_panel
    from_sibling = lax.ppermute(own_panel, "chan", [(c + 1, c) for c in range(0, n_chan, 2)])
    from_forward = lax.ppermute(second_panel, "chan", [(c - 1, c) for c in range(1, n_chan, 2)])
    odd = lax.axis_index("chan") % 2 == 1
    upper_panel = jnp.where(odd, from_forward, from_sibling)
    return upper_panel, second_panel, from_sibling


def shards(records, offsets, dead_mask, band_blocks):
    n_freq = lax.axis_size("freq")
    per_device = BINS // n_freq
    chunks = 2
    per_chunk = per_device // chunks
    table = dft_table(SEG_LEN, BINS, FIRST_BIN).reshape(n_freq, chunks, per_chunk, 2, SEG_LEN)
    table = table.transpose(3, 1, 0, 2, 4).reshape(2 * BINS, SEG_LEN)
    per_segment = whitened_spectra(records, offsets, dead_mask, table)
    seg_count, rows, channels = per_segment.shape
    slabs = per_segment.reshape(seg_count, 2, chunks, n_freq * per_chunk, channels)
    parts = [slabs[:, :, k].transpose(2, 1, 0, 3) for k in range(chunks)]
    chunk_products = []
    for k in range(chunks):
        own_panel = lax.all_to_all(parts[k], "freq", split_axis=0, concat_axis=2, tiled=True)
        upper_panel, second_panel, from_sibling = neighbour_panels(own_panel, merged=k + 1 == chunks)
        if k + 1 < chunks:
            _, parts[k + 1] = lax.optimization_barrier((from_sibling, parts[k + 1]))
        chunk_products.append(local_products(own_panel, [own_panel, upper_panel, second_panel]))
    band_limit = band_blocks[0]
    results = []
    for offset_index in range(BAND + 1):
        product = jnp.concatenate([p[offset_index] for p in chunk_products], axis=0)
        keep_flag = (offset_index <= band_limit).astype(jnp.bfloat16)
        results.append(product.astype(jnp.bfloat16) * keep_flag)
    return jnp.stack(results, axis=0)


def solution(mesh):
    in_specs = (P("freq", "chan"), P("freq"), P("chan"), P("chan"))
    out_specs = P(None, "freq", "chan", None)
    return jax.shard_map(shards, mesh=mesh, in_specs=in_specs, out_specs=out_specs, check_vma=False)
```
